128 devices in a mesh: expert: 32 (over y, x, core), pair: 4 (over z).
Axes of the slice: x: 4, y: 4, z: 4, core: 2. Of those that a mesh axis runs over, the one named last changes fastest.
Arguments:
- tokens: bfloat16 [16384, 4096], P(('expert', 'pair')), may hold values from -6 to 6
- expert_ids: int32 [16384, 8], P(('expert', 'pair')), may hold values from 0 to 127, all different within a row
- route_weight: float32 [16384, 8], P(('expert', 'pair')), may hold values from 0.1 to 1
- gate_weight: bfloat16 [32, 4096, 768], P('expert'), may hold values from -0.09375 to 0.09375
- up_weight: bfloat16 [32, 4096, 768], P('expert'), may hold values from -0.09375 to 0.09375
- down_weight: bfloat16 [32, 768, 4096], P('expert'), may hold values from -0.21875 to 0.21875
Outputs:
- combined: bfloat16 [16384, 4096], P(('expert', 'pair'))
- hessian: float32 [32, 768, 768], P('expert', 'pair')
- panel: float32 [32, 768, 128], P('expert', 'pair')
The draws below stay inside these ranges and needn't reach their ends.
Inputs may be any that keep to these rules, and one draw needn't show every extreme that they name: `expert_ids`: each row names 8 different experts, and every expert is named by some row.
All inputs are finite; a program needn't handle non-finite values.
Results may differ from the reference program's by a relative error of at most 0.0057.
Values may be sent and summed in bfloat16 or wider, within the bound.
No kernel may reach another device: no remote copies, remote signals or barrier semaphores. Data moves between devices by JAX's collectives and lax.ppermute only.
A program may use at most 128 MiB of HBM per device.

```python
import jax
import jax.numpy as jnp
from jax import lax

D = 4096
EXPERTS = 128
TOP = 8
FF = 768
PANEL = 128
TOK_DEV = 128
CAP = 16
FLIGHT = 32
TOKENS = 16384
N_EXPERT = 32
N_PAIR = 4


def levels(stream_key, extent, split, low, top_value):
    gain, own = 1.0, jax.random.fold_in(stream_key, 6)
    for dim, blocks in split:
        heights = jnp.exp(jax.random.uniform(jax.random.fold_in(own, dim), (blocks,), jnp.float32, low / len(split), top_value / len(split)))
        gain = gain * jnp.repeat(heights, extent[dim] // blocks).reshape([-1 if axis == dim else 1 for axis in range(len(extent))])
    return gain


def picks_of(rng, rows, number_of, top, lift):
    ranking = jax.random.permutation(jax.random.fold_in(rng, 1), number_of)
    pull = ranking
    for power in range(3):
        pull = pull * pull // number_of
    pull = pull * lift // number_of
    tickets = jax.random.randint(jax.random.fold_in(rng, 2), (rows, number_of), 0, 4096) + pull
    holders = jax.random.permutation(jax.random.fold_in(rng, 3), rows)[jnp.arange(number_of) % rows]
    tickets = jnp.where(jnp.arange(rows)[:, None] == holders[None, :], 1 << 14, tickets)
    merit = tickets * number_of + jnp.arange(number_of)
    return lax.top_k(merit.astype(jnp.int32), top)[1].astype(jnp.int32)


def normal_values(rng, extent, spread, most, shards=(), kind=jnp.bfloat16):
    values = jax.random.normal(rng, extent, jnp.float32) * spread
    if len(shards) > 0:
        values = levels(rng, extent, shards, -0.22, 0.18) * values
    return jnp.clip(values, min=-most, max=most).astype(kind)


def setup_inputs(seed: int = 0) -> dict:
    streams_of = jax.random.split(jax.random.key(seed), 7)
    return {
        "tokens": normal_values(streams_of[0], (TOKENS, D), 1.0, 6.0, ((0, 128),)),
        "expert_ids": picks_of(streams_of[1], TOKENS, EXPERTS, TOP, 1024),
        "route_weight": jnp.clip(0.1 + 0.9 * jax.random.uniform(streams_of[2], (TOKENS, TOP), jnp.float32) ** levels(streams_of[2], (TOKENS, TOP), ((0, 128),), -0.2, 0.2), 0.1, 1.0),
        "gate_weight": normal_values(streams_of[3], (FLIGHT, D, FF), D ** -0.5, 0.09375, ((0, 32),)),
        "up_weight": normal_values(streams_of[4], (FLIGHT, D, FF), D ** -0.5, 0.09375, ((0, 32),)),
        "down_weight": normal_values(streams_of[5], (FLIGHT, FF, D), FF ** -0.5, 0.21875, ((0, 32),)),
    }


def reference(tokens, expert_ids, route_weight, gate_weight, up_weight, down_weight):
    per_owner = EXPERTS // N_EXPERT
    sources = N_EXPERT * N_PAIR
    slot_total = sources * CAP
    grouped = expert_ids.reshape(sources, TOK_DEV, TOP)
    in_flight = grouped % per_owner == 0
    owner_of = grouped // per_owner
    columns = jnp.arange(N_EXPERT, dtype=jnp.int32)
    route_hit = (in_flight[..., None] & (owner_of[..., None] == columns)).astype(jnp.int32)
    picked = jnp.sum(route_hit, axis=2)
    before = jnp.cumsum(picked, axis=1) - picked
    kept_rows = picked * (before < CAP).astype(jnp.int32)
    rank_choice = jnp.sum(route_hit * before[:, :, None, :], axis=3)
    keep_choice = jnp.sum(route_hit * kept_rows[:, :, None, :], axis=3)
    source_ids = jnp.arange(sources, dtype=jnp.int32)[:, None, None]
    token_ids = source_ids * TOK_DEV + jnp.arange(TOK_DEV, dtype=jnp.int32)[None, :, None]
    token_ids = jnp.broadcast_to(token_ids, grouped.shape).astype(jnp.int32)
    position = owner_of * slot_total + source_ids * CAP + rank_choice
    position = jnp.where(keep_choice > 0, position, N_EXPERT * slot_total).astype(jnp.int32)
    flat_position = position.reshape(-1)
    row_table = jnp.full((N_EXPERT * slot_total,), -1, jnp.int32).at[flat_position].set(token_ids.reshape(-1), mode='drop')
    weight_table = jnp.zeros((N_EXPERT * slot_total,), jnp.float32).at[flat_position].set(route_weight.reshape(-1), mode='drop')
    hess_scale = 2.0 / (CAP * N_EXPERT * N_PAIR)
    corner_identity = jnp.eye(PANEL, dtype=jnp.float32)
    lead_identity = jnp.eye(FF, PANEL, dtype=jnp.float32)

    def one_expert(accumulated, inputs):
        row_ids, row_weights, gate_matrix, upper_matrix, down_matrix = inputs
        valid_rows = row_ids >= 0
        safe_ids = jnp.maximum(row_ids, 0).astype(jnp.int32)
        gathered = jnp.where(valid_rows[:, None], tokens[safe_ids], jnp.zeros((), tokens.dtype))
        gate_value = jnp.dot(gathered.astype(jnp.float32), gate_matrix.astype(jnp.float32), preferred_element_type=jnp.float32)
        upper_value = jnp.dot(gathered.astype(jnp.float32), upper_matrix.astype(jnp.float32), preferred_element_type=jnp.float32)
        hidden = (jax.nn.silu(gate_value) * upper_value).astype(jnp.bfloat16)
        output = jnp.dot(hidden.astype(jnp.float32), down_matrix.astype(jnp.float32), preferred_element_type=jnp.float32).astype(jnp.bfloat16)
        hessian = lax.dot_general(hidden.astype(jnp.float32), hidden.astype(jnp.float32), (((0,), (0,)), ((), ())), preferred_element_type=jnp.float32) * hess_scale
        damping = 0.01 * jnp.trace(hessian) / FF
        lower_factor = jnp.linalg.cholesky(hessian[:PANEL, :PANEL] + damping * corner_identity)
        leading = hessian[:, :PANEL] + damping * lead_identity
        panel_rows = jax.scipy.linalg.solve_triangular(lower_factor, leading.T, lower=True).T
        accumulated = accumulated.at[safe_ids].add(row_weights[:, None] * output.astype(jnp.float32))
        return (accumulated, (hessian, panel_rows))
    initial = jnp.zeros((TOKENS, D), jnp.float32)
    inputs = (row_table.reshape(N_EXPERT, slot_total), weight_table.reshape(N_EXPERT, slot_total), gate_weight, up_weight, down_weight)
    accumulated, (hessians, panels) = lax.scan(one_expert, initial, inputs)
    return (accumulated.astype(jnp.bfloat16), hessians, panels)
```

```python
import jax
import jax.numpy as jnp
from jax import lax
from jax.sharding import PartitionSpec as P

EXPERTS = 128
FF = 768
PANEL = 128
CAP = 16


def swiglu_rows(flat_rows, gate_matrix, upper_matrix, down_matrix):
    gate_value = jnp.dot(flat_rows, gate_matrix, preferred_element_type=jnp.float32)
    upper_value = jnp.dot(flat_rows, upper_matrix, preferred_element_type=jnp.float32)
    hidden = (jax.nn.silu(gate_value) * upper_value).astype(jnp.bfloat16)
    output = jnp.dot(hidden, down_matrix, preferred_element_type=jnp.float32).astype(jnp.bfloat16)
    return (hidden, output)


def split_bf16(values):
    high = values.astype(jnp.bfloat16)
    low = (values - high.astype(jnp.float32)).astype(jnp.bfloat16)
    return high, low


def per_device(tokens, expert_ids, route_weight, gate_weight, up_weight, down_weight):
    owners = lax.axis_size("expert")
    pair_count = lax.axis_size("pair")
    tok_count = tokens.shape[0]
    model_width = tokens.shape[1]
    per_owner = EXPERTS // owners
    in_flight = expert_ids % per_owner == 0
    owner_of = expert_ids // per_owner
    columns = lax.broadcasted_iota(jnp.int32, (1, 1, owners), 2)
    route_hit = (in_flight[:, :, None] & (owner_of[:, :, None] == columns)).astype(jnp.int32)
    picked = jnp.sum(route_hit, axis=1)
    before = jnp.cumsum(picked, axis=0) - picked
    kept_rows = picked * (before < CAP).astype(jnp.int32)
    slot_ids = lax.broadcasted_iota(jnp.int32, (1, 1, CAP), 2)
    slot_marks = kept_rows[:, :, None] * (before[:, :, None] == slot_ids).astype(jnp.int32)
    marks_flat = slot_marks.reshape(tok_count, owners * CAP)
    selector = marks_flat.astype(jnp.bfloat16)
    outgoing = lax.dot_general(
        selector, tokens, (((0,), (0,)), ((), ())), preferred_element_type=jnp.float32
    ).astype(jnp.bfloat16)
    outgoing = outgoing.reshape(owners, CAP, model_width)
    gate_matrix = gate_weight[0]
    upper_matrix = up_weight[0]
    down_matrix = down_weight[0]
    arrived = lax.all_to_all(outgoing, "expert", split_axis=0, concat_axis=0, tiled=True)
    item_count = arrived.shape[1]
    hidden, output = swiglu_rows(
        arrived.reshape(-1, model_width), gate_matrix, upper_matrix, down_matrix
    )
    results = output.reshape(owners, item_count, model_width)
    returned = lax.all_to_all(results, "expert", split_axis=0, concat_axis=0, tiled=True)
    returned_flat = returned.reshape(-1, model_width)
    owner_weight = jnp.sum(route_hit.astype(jnp.float32) * route_weight[:, :, None], axis=1)
    combine_matrix = (
        slot_marks.astype(jnp.float32) * owner_weight[:, :, None]
    ).reshape(tok_count, owners * CAP)
    weight_high, weight_low = split_bf16(combine_matrix)
    combined = jnp.dot(weight_high, returned_flat, preferred_element_type=jnp.float32) + jnp.dot(
        weight_low, returned_flat, preferred_element_type=jnp.float32
    )
    hess_scale = 2.0 / (CAP * owners * pair_count)
    all_hidden = lax.all_gather(hidden, "pair", axis=0, tiled=True)
    whole_sum = (
        lax.dot_general(
            all_hidden, all_hidden, (((0,), (0,)), ((), ())), preferred_element_type=jnp.float32
        )
        * hess_scale
    )
    row_share = FF // pair_count
    pair_place = lax.axis_index("pair")
    damping = 0.01 * jnp.trace(whole_sum) / FF
    corner = whole_sum[:PANEL, :PANEL]
    my_rows = lax.dynamic_slice_in_dim(whole_sum, pair_place * row_share, row_share, 0)
    lower_factor = jnp.linalg.cholesky(corner + damping * jnp.eye(PANEL, dtype=jnp.float32))
    row_ids = pair_place * row_share + lax.broadcasted_iota(jnp.int32, (row_share, PANEL), 0)
    column_ids = lax.broadcasted_iota(jnp.int32, (row_share, PANEL), 1)
    leading = my_rows[:, :PANEL] + damping * (row_ids == column_ids).astype(jnp.float32)
    panel_rows = jax.scipy.linalg.solve_triangular(lower_factor, leading.T, lower=True).T
    return (combined.astype(jnp.bfloat16), my_rows[None], panel_rows[None])


def solution(mesh):
    in_specs = (
        P(("expert", "pair"), None),
        P(("expert", "pair"), None),
        P(("expert", "pair"), None),
        P("expert", None, None),
        P("expert", None, None),
        P("expert", None, None),
    )
    out_specs = (P(("expert", "pair"), None), P("expert", "pair", None), P("expert", "pair", None))
    return jax.shard_map(
        per_device, mesh=mesh, in_specs=in_specs, out_specs=out_specs, check_vma=False
    )
```

```python
import jax
import jax.numpy as jnp
from jax import lax
from jax.sharding import PartitionSpec as P

EXPERTS = 128
FF = 768
PANEL = 128
CAP = 16


def swiglu_rows(flat_rows, gate_matrix, upper_matrix, down_matrix):
    gate_value = jnp.dot(flat_rows, gate_matrix, preferred_element_type=jnp.float32)
    upper_value = jnp.dot(flat_rows, upper_matrix, preferred_element_type=jnp.float32)
    hidden = (jax.nn.silu(gate_value) * upper_value).astype(jnp.bfloat16)
    output = jnp.dot(hidden, down_matrix, preferred_element_type=jnp.float32).astype(jnp.bfloat16)
    return (hidden, output)


def split_bf16(values):
    high = values.astype(jnp.bfloat16)
    low = (values - high.astype(jnp.float32)).astype(jnp.bfloat16)
    return high, low


def per_device(tokens, expert_ids, route_weight, gate_weight, up_weight, down_weight):
    owners = lax.axis_size("expert")
    pair_count = lax.axis_size("pair")
    tok_count = tokens.shape[0]
    model_width = tokens.shape[1]
    per_owner = EXPERTS // owners
    in_flight = expert_ids % per_owner == 0
    owner_of = expert_ids // per_owner
    columns = lax.broadcasted_iota(jnp.int32, (1, 1, owners), 2)
    route_hit = (in_flight[:, :, None] & (owner_of[:, :, None] == columns)).astype(jnp.int32)
    picked = jnp.sum(route_hit, axis=1)
    before = jnp.cumsum(picked, axis=0) - picked
    kept_rows = picked * (before < CAP).astype(jnp.int32)
    slot_ids = lax.broadcasted_iota(jnp.int32, (1, 1, CAP), 2)
    slot_marks = kept_rows[:, :, None] * (before[:, :, None] == slot_ids).astype(jnp.int32)
    marks_flat = slot_marks.reshape(tok_count, owners * CAP)
    selector = marks_flat.astype(jnp.bfloat16)
    outgoing = lax.dot_general(
        selector, tokens, (((0,), (0,)), ((), ())), preferred_element_type=jnp.float32
    ).astype(jnp.bfloat16)
    outgoing = outgoing.reshape(owners, CAP, model_width)
    gate_matrix = gate_weight[0]
    upper_matrix = up_weight[0]
    down_matrix = down_weight[0]
    arrived = lax.all_to_all(outgoing, "expert", split_axis=0, concat_axis=0, tiled=True)
    item_count = arrived.shape[1]
    hidden, output = swiglu_rows(
        arrived.reshape(-1, model_width), gate_matrix, upper_matrix, down_matrix
    )
    results = output.reshape(owners, item_count, model_width)
    returned = lax.all_to_all(results, "expert", split_axis=0, concat_axis=0, tiled=True)
    returned_flat = returned.reshape(-1, model_width)
    owner_weight = jnp.sum(route_hit.astype(jnp.float32) * route_weight[:, :, None], axis=1)
    combine_matrix = (
        slot_marks.astype(jnp.float32) * owner_weight[:, :, None]
    ).reshape(tok_count, owners * CAP)
    weight_high, weight_low = split_bf16(combine_matrix)
    combined = jnp.dot(weight_high, returned_flat, preferred_element_type=jnp.float32) + jnp.dot(
        weight_low, returned_flat, preferred_element_type=jnp.float32
    )
    hess_scale = 2.0 / (CAP * owners * pair_count)
    row_share = FF // pair_count
    pair_place = lax.axis_index("pair")
    hidden_wide = hidden.astype(jnp.float32)
    corner_part = lax.dot_general(
        hidden[:, :PANEL], hidden[:, :PANEL], (((0,), (0,)), ((), ())),
        preferred_element_type=jnp.float32,
    )
    square_part = jnp.broadcast_to(jnp.sum(hidden_wide * hidden_wide), (8, PANEL))
    pack = jnp.concatenate([corner_part, square_part], axis=0)
    pack_sum = pack
    for shift in range(1, pair_count):
        ring = [(i, (i + shift) % pair_count) for i in range(pair_count)]
        pack_sum = pack_sum + lax.ppermute(pack, "pair", ring)
    corner = pack_sum[:PANEL] * hess_scale
    damping = 0.01 * (pack_sum[PANEL, 0] * hess_scale) / FF
    lower_factor = jnp.linalg.cholesky(corner + damping * jnp.eye(PANEL, dtype=jnp.float32))
    all_hidden = lax.all_gather(hidden, "pair", axis=0, tiled=True)
    my_columns = lax.dynamic_slice_in_dim(all_hidden, pair_place * row_share, row_share, 1)
    my_rows = (
        lax.dot_general(
            my_columns, all_hidden, (((0,), (0,)), ((), ())), preferred_element_type=jnp.float32
        )
        * hess_scale
    )
    row_ids = pair_place * row_share + lax.broadcasted_iota(jnp.int32, (row_share, PANEL), 0)
    column_ids = lax.broadcasted_iota(jnp.int32, (row_share, PANEL), 1)
    leading = my_rows[:, :PANEL] + damping * (row_ids == column_ids).astype(jnp.float32)
    panel_rows = jax.scipy.linalg.solve_triangular(lower_factor, leading.T, lower=True).T
    return (combined.astype(jnp.bfloat16), my_rows[None], panel_rows[None])


def solution(mesh):
    in_specs = (
        P(("expert", "pair"), None),
        P(("expert", "pair"), None),
        P(("expert", "pair"), None),
        P("expert", None, None),
        P("expert", None, None),
        P("expert", None, None),
    )
    out_specs = (P(("expert", "pair"), None), P("expert", "pair", None), P("expert", "pair", None))
    return jax.shard_map(
        per_device, mesh=mesh, in_specs=in_specs, out_specs=out_specs, check_vma=False
    )
```

```python
import jax
import jax.numpy as jnp
from jax import lax
from jax.sharding import PartitionSpec as P

EXPERTS = 128
FF = 768
PANEL = 128
CAP = 16
CHUNKS = 2


def swiglu_rows(flat_rows, gate_matrix, upper_matrix, down_matrix):
    gate_value = jnp.dot(flat_rows, gate_matrix, preferred_element_type=jnp.float32)
    upper_value = jnp.dot(flat_rows, upper_matrix, preferred_element_type=jnp.float32)
    hidden = (jax.nn.silu(gate_value) * upper_value).astype(jnp.bfloat16)
    output = jnp.dot(hidden, down_matrix, preferred_element_type=jnp.float32).astype(jnp.bfloat16)
    return (hidden, output)


def split_bf16(values):
    rounded = lax.reduce_precision(values, exponent_bits=8, mantissa_bits=7)
    return rounded.astype(jnp.bfloat16), (values - rounded).astype(jnp.bfloat16)


def per_device(tokens, expert_ids, route_weight, gate_weight, up_weight, down_weight):
    owners = lax.axis_size("expert")
    pair_count = lax.axis_size("pair")
    tok_count = tokens.shape[0]
    model_width = tokens.shape[1]
    per_owner = EXPERTS // owners
    in_flight = expert_ids % per_owner == 0
    owner_of = expert_ids // per_owner
    columns = lax.broadcasted_iota(jnp.int32, (1, 1, owners), 2)
    route_hit = (in_flight[:, :, None] & (owner_of[:, :, None] == columns)).astype(jnp.int32)
    picked = jnp.sum(route_hit, axis=1)
    before = jnp.cumsum(picked, axis=0) - picked
    kept_rows = picked * (before < CAP).astype(jnp.int32)
    slot_ids = lax.broadcasted_iota(jnp.int32, (1, 1, CAP), 2)
    slot_marks = kept_rows[:, :, None] * (before[:, :, None] == slot_ids).astype(jnp.int32)
    gate_matrix = gate_weight[0]
    upper_matrix = up_weight[0]
    down_matrix = down_weight[0]
    owner_weight = jnp.sum(route_hit.astype(jnp.float32) * route_weight[:, :, None], axis=1)
    combine_weights = slot_marks.astype(jnp.float32) * owner_weight[:, :, None]
    chunk = CAP // CHUNKS
    combined = jnp.zeros((tok_count, model_width), jnp.float32)
    hidden_parts = []
    for part in range(CHUNKS):
        marks_part = slot_marks[:, :, part * chunk : (part + 1) * chunk]
        selector = marks_part.reshape(tok_count, owners * chunk).astype(jnp.bfloat16)
        outgoing = lax.dot_general(
            selector, tokens, (((0,), (0,)), ((), ())), preferred_element_type=jnp.float32
        ).astype(jnp.bfloat16)
        outgoing = outgoing.reshape(owners, chunk, model_width)
        arrived = lax.all_to_all(outgoing, "expert", split_axis=0, concat_axis=0, tiled=True)
        hidden, output = swiglu_rows(
            arrived.reshape(-1, model_width), gate_matrix, upper_matrix, down_matrix
        )
        hidden_parts.append(hidden)
        results = output.reshape(owners, chunk, model_width)
        returned = lax.all_to_all(results, "expert", split_axis=0, concat_axis=0, tiled=True)
        returned_flat = returned.reshape(-1, model_width)
        weights_part = combine_weights[:, :, part * chunk : (part + 1) * chunk]
        weight_high, weight_low = split_bf16(weights_part.reshape(tok_count, owners * chunk))
        combined = combined + jnp.dot(
            weight_high, returned_flat, preferred_element_type=jnp.float32
        ) + jnp.dot(weight_low, returned_flat, preferred_element_type=jnp.float32)
    hess_scale = 2.0 / (CAP * owners * pair_count)
    row_share = FF // pair_count
    pair_place = lax.axis_index("pair")
    corner_part = jnp.zeros((PANEL, PANEL), jnp.float32)
    square_sum = jnp.zeros((), jnp.float32)
    for hidden in hidden_parts:
        hidden_wide = hidden.astype(jnp.float32)
        corner_part = corner_part + lax.dot_general(
            hidden[:, :PANEL], hidden[:, :PANEL], (((0,), (0,)), ((), ())),
            preferred_element_type=jnp.float32,
        )
        square_sum = square_sum + jnp.sum(hidden_wide * hidden_wide)
    square_part = jnp.broadcast_to(square_sum, (8, PANEL))
    pack = jnp.concatenate([corner_part, square_part], axis=0)
    pack_sum = pack
    for shift in range(1, pair_count):
        ring = [(i, (i + shift) % pair_count) for i in range(pair_count)]
        pack_sum = pack_sum + lax.ppermute(pack, "pair", ring)
    corner = pack_sum[:PANEL] * hess_scale
    damping = 0.01 * (pack_sum[PANEL, 0] * hess_scale) / FF
    lower_factor = jnp.linalg.cholesky(corner + damping * jnp.eye(PANEL, dtype=jnp.float32))
    row_sum = jnp.zeros((row_share, FF), jnp.float32)
    for hidden in hidden_parts:
        all_hidden = lax.all_gather(hidden, "pair", axis=0, tiled=True)
        my_columns = lax.dynamic_slice_in_dim(all_hidden, pair_place * row_share, row_share, 1)
        row_sum = row_sum + lax.dot_general(
            my_columns, all_hidden, (((0,), (0,)), ((), ())), preferred_element_type=jnp.float32
        )
    my_rows = row_sum * hess_scale
    row_ids = pair_place * row_share + lax.broadcasted_iota(jnp.int32, (row_share, PANEL), 0)
    column_ids = lax.broadcasted_iota(jnp.int32, (row_share, PANEL), 1)
    leading = my_rows[:, :PANEL] + damping * (row_ids == column_ids).astype(jnp.float32)
    panel_rows = jax.scipy.linalg.solve_triangular(lower_factor, leading.T, lower=True).T
    return (combined.astype(jnp.bfloat16), my_rows[None], panel_rows[None])


def solution(mesh):
    in_specs = (
        P(("expert", "pair"), None),
        P(("expert", "pair"), None),
        P(("expert", "pair"), None),
        P("expert", None, None),
        P("expert", None, None),
        P("expert", None, None),
    )
    out_specs = (P(("expert", "pair"), None), P("expert", "pair", None), P("expert", "pair", None))
    return jax.shard_map(
        per_device, mesh=mesh, in_specs=in_specs, out_specs=out_specs, check_vma=False
    )
```

```python
import jax
import jax.numpy as jnp
from jax import lax
from jax.sharding import PartitionSpec as P

EXPERTS = 128
FF = 768
PANEL = 128
CAP = 16


def swiglu_rows(flat_rows, gate_matrix, upper_matrix, down_matrix):
    gate_value = jnp.dot(flat_rows, gate_matrix, preferred_element_type=jnp.float32)
    upper_value = jnp.dot(flat_rows, upper_matrix, preferred_element_type=jnp.float32)
    hidden = (jax.nn.silu(gate_value) * upper_value).astype(jnp.bfloat16)
    output = jnp.dot(hidden, down_matrix, preferred_element_type=jnp.float32).astype(jnp.bfloat16)
    return (hidden, output)


def split_bf16(values):
    rounded = lax.reduce_precision(values, exponent_bits=8, mantissa_bits=7)
    return rounded.astype(jnp.bfloat16), (values - rounded).astype(jnp.bfloat16)


def per_device(tokens, expert_ids, route_weight, gate_weight, up_weight, down_weight):
    owners = lax.axis_size("expert")
    pair_count = lax.axis_size("pair")
    tok_count = tokens.shape[0]
    model_width = tokens.shape[1]
    per_owner = EXPERTS // owners
    in_flight = expert_ids % per_owner == 0
    owner_of = expert_ids // per_owner
    columns = lax.broadcasted_iota(jnp.int32, (1, 1, owners), 2)
    route_hit = (in_flight[:, :, None] & (owner_of[:, :, None] == columns)).astype(jnp.int32)
    picked = jnp.sum(route_hit, axis=1)
    before = jnp.cumsum(picked, axis=0) - picked
    kept_rows = picked * (before < CAP).astype(jnp.int32)
    slot_ids = lax.broadcasted_iota(jnp.int32, (1, 1, CAP), 2)
    slot_marks = kept_rows[:, :, None] * (before[:, :, None] == slot_ids).astype(jnp.int32)
    marks_flat = slot_marks.reshape(tok_count, owners * CAP)
    selector = marks_flat.astype(jnp.bfloat16)
    outgoing = lax.dot_general(
        selector, tokens, (((0,), (0,)), ((), ())), preferred_element_type=jnp.float32
    ).astype(jnp.bfloat16)
    outgoing = outgoing.reshape(owners, CAP, model_width)
    gate_matrix = gate_weight[0]
    upper_matrix = up_weight[0]
    down_matrix = down_weight[0]
    arrived = lax.all_to_all(outgoing, "expert", split_axis=0, concat_axis=0, tiled=True)
    item_count = arrived.shape[1]
    hidden, output = swiglu_rows(
        arrived.reshape(-1, model_width), gate_matrix, upper_matrix, down_matrix
    )
    results = output.reshape(owners, item_count, model_width)
    returned = lax.all_to_all(results, "expert", split_axis=0, concat_axis=0, tiled=True)
    returned_flat = returned.reshape(-1, model_width)
    owner_weight = jnp.sum(route_hit.astype(jnp.float32) * route_weight[:, :, None], axis=1)
    combine_matrix = (
        slot_marks.astype(jnp.float32) * owner_weight[:, :, None]
    ).reshape(tok_count, owners * CAP)
    weight_high, weight_low = split_bf16(combine_matrix)
    combined = jnp.dot(weight_high, returned_flat, preferred_element_type=jnp.float32) + jnp.dot(
        weight_low, returned_flat, preferred_element_type=jnp.float32
    )
    hess_scale = 2.0 / (CAP * owners * pair_count)
    row_share = FF // pair_count
    pair_place = lax.axis_index("pair")
    hidden_wide = hidden.astype(jnp.float32)
    corner_part = lax.dot_general(
        hidden[:, :PANEL], hidden[:, :PANEL], (((0,), (0,)), ((), ())),
        preferred_element_type=jnp.float32,
    )
    square_part = jnp.broadcast_to(jnp.sum(hidden_wide * hidden_wide), (8, PANEL))
    pack = jnp.concatenate([corner_part, square_part], axis=0)
    pack_sum = pack
    for shift in range(1, pair_count):
        ring = [(i, (i + shift) % pair_count) for i in range(pair_count)]
        pack_sum = pack_sum + lax.ppermute(pack, "pair", ring)
    corner = pack_sum[:PANEL] * hess_scale
    damping = 0.01 * (pack_sum[PANEL, 0] * hess_scale) / FF
    lower_factor = jnp.linalg.cholesky(corner + damping * jnp.eye(PANEL, dtype=jnp.float32))
    gathered = [hidden]
    for shift in range(1, pair_count):
        ring = [(i, (i + shift) % pair_count) for i in range(pair_count)]
        gathered.append(lax.ppermute(hidden, "pair", ring))
    all_hidden = jnp.concatenate(gathered, axis=0)
    my_columns = lax.dynamic_slice_in_dim(all_hidden, pair_place * row_share, row_share, 1)
    my_rows = (
        lax.dot_general(
            my_columns, all_hidden, (((0,), (0,)), ((), ())), preferred_element_type=jnp.float32
        )
        * hess_scale
    )
    row_ids = pair_place * row_share + lax.broadcasted_iota(jnp.int32, (row_share, PANEL), 0)
    column_ids = lax.broadcasted_iota(jnp.int32, (row_share, PANEL), 1)
    leading = my_rows[:, :PANEL] + damping * (row_ids == column_ids).astype(jnp.float32)
    panel_rows = jax.scipy.linalg.solve_triangular(lower_factor, leading.T, lower=True).T
    return (combined.astype(jnp.bfloat16), my_rows[None], panel_rows[None])


def solution(mesh):
    in_specs = (
        P(("expert", "pair"), None),
        P(("expert", "pair"), None),
        P(("expert", "pair"), None),
        P("expert", None, None),
        P("expert", None, None),
        P("expert", None, None),
    )
    out_specs = (P(("expert", "pair"), None), P("expert", "pair", None), P("expert", "pair", None))
    return jax.shard_map(
        per_device, mesh=mesh, in_specs=in_specs, out_specs=out_specs, check_vma=False
    )
```

```python
import jax
import jax.numpy as jnp
from jax import lax
from jax.sharding import PartitionSpec as P
from jax.experimental import pallas as pl
from jax.experimental.pallas import tpu as pltpu

EXPERTS = 128
FF = 768
PANEL = 128
CAP = 16


def swiglu_rows(flat_rows, gate_matrix, upper_matrix, down_matrix):
    gate_value = jnp.dot(flat_rows, gate_matrix, preferred_element_type=jnp.float32)
    upper_value = jnp.dot(flat_rows, upper_matrix, preferred_element_type=jnp.float32)
    hidden = (jax.nn.silu(gate_value) * upper_value).astype(jnp.bfloat16)
    output = jnp.dot(hidden, down_matrix, preferred_element_type=jnp.float32).astype(jnp.bfloat16)
    return (hidden, output)


def split_bf16(values):
    rounded = lax.reduce_precision(values, exponent_bits=8, mantissa_bits=7)
    return rounded.astype(jnp.bfloat16), (values - rounded).astype(jnp.bfloat16)


def combine_kernel(high_ref, low_ref, rows_ref, out_ref):
    rows = rows_ref[...]
    total = jnp.dot(high_ref[...], rows, preferred_element_type=jnp.float32)
    total = total + jnp.dot(low_ref[...], rows, preferred_element_type=jnp.float32)
    out_ref[...] = total.astype(out_ref.dtype)


def combine_rows(weight_high, weight_low, rows):
    tok_count, slot_count = weight_high.shape
    width = rows.shape[1]
    block = 1024
    return pl.pallas_call(
        combine_kernel,
        out_shape=jax.ShapeDtypeStruct((tok_count, width), jnp.bfloat16),
        grid=(width // block,),
        in_specs=[
            pl.BlockSpec((tok_count, slot_count), lambda j: (0, 0)),
            pl.BlockSpec((tok_count, slot_count), lambda j: (0, 0)),
            pl.BlockSpec((slot_count, block), lambda j: (0, j)),
        ],
        out_specs=pl.BlockSpec((tok_count, block), lambda j: (0, j)),
        cost_estimate=pl.CostEstimate(
            flops=4 * tok_count * slot_count * width,
            transcendentals=0,
            bytes_accessed=2 * (slot_count * width + tok_count * width + 2 * tok_count * slot_count),
        ),
    )(weight_high, weight_low, rows)


def per_device(tokens, expert_ids, route_weight, gate_weight, up_weight, down_weight):
    owners = lax.axis_size("expert")
    pair_count = lax.axis_size("pair")
    tok_count = tokens.shape[0]
    model_width = tokens.shape[1]
    per_owner = EXPERTS // owners
    in_flight = expert_ids % per_owner == 0
    owner_of = expert_ids // per_owner
    columns = lax.broadcasted_iota(jnp.int32, (1, 1, owners), 2)
    route_hit = (in_flight[:, :, None] & (owner_of[:, :, None] == columns)).astype(jnp.int32)
    picked = jnp.sum(route_hit, axis=1)
    before = jnp.cumsum(picked, axis=0) - picked
    kept_rows = picked * (before < CAP).astype(jnp.int32)
    slot_ids = lax.broadcasted_iota(jnp.int32, (1, 1, CAP), 2)
    slot_marks = kept_rows[:, :, None] * (before[:, :, None] == slot_ids).astype(jnp.int32)
    marks_flat = slot_marks.reshape(tok_count, owners * CAP)
    selector = marks_flat.astype(jnp.bfloat16)
    outgoing = lax.dot_general(
        selector, tokens, (((0,), (0,)), ((), ())), preferred_element_type=jnp.float32
    ).astype(jnp.bfloat16)
    outgoing = outgoing.reshape(owners, CAP, model_width)
    gate_matrix = gate_weight[0]
    upper_matrix = up_weight[0]
    down_matrix = down_weight[0]
    arrived = lax.all_to_all(outgoing, "expert", split_axis=0, concat_axis=0, tiled=True)
    item_count = arrived.shape[1]
    hidden, output = swiglu_rows(
        arrived.reshape(-1, model_width), gate_matrix, upper_matrix, down_matrix
    )
    results = output.reshape(owners, item_count, model_width)
    returned = lax.all_to_all(results, "expert", split_axis=0, concat_axis=0, tiled=True)
    returned_flat = returned.reshape(-1, model_width)
    owner_weight = jnp.sum(route_hit.astype(jnp.float32) * route_weight[:, :, None], axis=1)
    combine_matrix = (
        slot_marks.astype(jnp.float32) * owner_weight[:, :, None]
    ).reshape(tok_count, owners * CAP)
    weight_high, weight_low = split_bf16(combine_matrix)
    combined = combine_rows(weight_high, weight_low, returned_flat)
    hess_scale = 2.0 / (CAP * owners * pair_count)
    row_share = FF // pair_count
    pair_place = lax.axis_index("pair")
    hidden_wide = hidden.astype(jnp.float32)
    corner_part = lax.dot_general(
        hidden[:, :PANEL], hidden[:, :PANEL], (((0,), (0,)), ((), ())),
        preferred_element_type=jnp.float32,
    )
    square_part = jnp.broadcast_to(jnp.sum(hidden_wide * hidden_wide), (8, PANEL))
    pack = jnp.concatenate([corner_part, square_part], axis=0)
    pack_sum = pack
    for shift in range(1, pair_count):
        ring = [(i, (i + shift) % pair_count) for i in range(pair_count)]
        pack_sum = pack_sum + lax.ppermute(pack, "pair", ring)
    corner = pack_sum[:PANEL] * hess_scale
    damping = 0.01 * (pack_sum[PANEL, 0] * hess_scale) / FF
    lower_factor = jnp.linalg.cholesky(corner + damping * jnp.eye(PANEL, dtype=jnp.float32))
    gathered = [hidden]
    for shift in range(1, pair_count):
        ring = [(i, (i + shift) % pair_count) for i in range(pair_count)]
        gathered.append(lax.ppermute(hidden, "pair", ring))
    all_hidden = jnp.concatenate(gathered, axis=0)
    my_columns = lax.dynamic_slice_in_dim(all_hidden, pair_place * row_share, row_share, 1)
    my_rows = (
        lax.dot_general(
            my_columns, all_hidden, (((0,), (0,)), ((), ())), preferred_element_type=jnp.float32
        )
        * hess_scale
    )
    row_ids = pair_place * row_share + lax.broadcasted_iota(jnp.int32, (row_share, PANEL), 0)
    column_ids = lax.broadcasted_iota(jnp.int32, (row_share, PANEL), 1)
    leading = my_rows[:, :PANEL] + damping * (row_ids == column_ids).astype(jnp.float32)
    panel_rows = jax.scipy.linalg.solve_triangular(lower_factor, leading.T, lower=True).T
    return (combined, my_rows[None], panel_rows[None])


def solution(mesh):
    in_specs = (
        P(("expert", "pair"), None),
        P(("expert", "pair"), None),
        P(("expert", "pair"), None),
        P("expert", None, None),
        P("expert", None, None),
        P("expert", None, None),
    )
    out_specs = (P(("expert", "pair"), None), P("expert", "pair", None), P("expert", "pair", None))
    return jax.shard_map(
        per_device, mesh=mesh, in_specs=in_specs, out_specs=out_specs, check_vma=False
    )
```

```python
import jax
import jax.numpy as jnp
from jax import lax
from jax.sharding import PartitionSpec as P
from jax.experimental import pallas as pl
from jax.experimental.pallas import tpu as pltpu

EXPERTS = 128
FF = 768
PANEL = 128
CAP = 16


def swiglu_rows(flat_rows, gate_matrix, upper_matrix, down_matrix):
    gate_value = jnp.dot(flat_rows, gate_matrix, preferred_element_type=jnp.float32)
    upper_value = jnp.dot(flat_rows, upper_matrix, preferred_element_type=jnp.float32)
    hidden = (jax.nn.silu(gate_value) * upper_value).astype(jnp.bfloat16)
    output = jnp.dot(hidden, down_matrix, preferred_element_type=jnp.float32).astype(jnp.bfloat16)
    return (hidden, output)


def split_bf16(values):
    rounded = lax.reduce_precision(values, exponent_bits=8, mantissa_bits=7)
    return rounded.astype(jnp.bfloat16), (values - rounded).astype(jnp.bfloat16)


def combine_kernel(high_ref, low_ref, rows_ref, out_ref):
    rows = rows_ref[...]
    total = jnp.dot(high_ref[...], rows, preferred_element_type=jnp.float32)
    total = total + jnp.dot(low_ref[...], rows, preferred_element_type=jnp.float32)
    out_ref[...] = total.astype(out_ref.dtype)


def combine_rows(weight_high, weight_low, rows):
    tok_count, slot_count = weight_high.shape
    width = rows.shape[1]
    block = 1024
    return pl.pallas_call(
        combine_kernel,
        out_shape=jax.ShapeDtypeStruct((tok_count, width), jnp.bfloat16),
        grid=(width // block,),
        in_specs=[
            pl.BlockSpec((tok_count, slot_count), lambda j: (0, 0)),
            pl.BlockSpec((tok_count, slot_count), lambda j: (0, 0)),
            pl.BlockSpec((slot_count, block), lambda j: (0, j)),
        ],
        out_specs=pl.BlockSpec((tok_count, block), lambda j: (0, j)),
        cost_estimate=pl.CostEstimate(
            flops=4 * tok_count * slot_count * width,
            transcendentals=0,
            bytes_accessed=2 * (slot_count * width + tok_count * width + 2 * tok_count * slot_count),
        ),
    )(weight_high, weight_low, rows)


def per_device(tokens, expert_ids, route_weight, gate_weight, up_weight, down_weight):
    owners = lax.axis_size("expert")
    pair_count = lax.axis_size("pair")
    tok_count = tokens.shape[0]
    model_width = tokens.shape[1]
    per_owner = EXPERTS // owners
    in_flight = expert_ids % per_owner == 0
    owner_of = expert_ids // per_owner
    columns = lax.broadcasted_iota(jnp.int32, (1, 1, owners), 2)
    route_hit = (in_flight[:, :, None] & (owner_of[:, :, None] == columns)).astype(jnp.int32)
    picked = jnp.sum(route_hit, axis=1)
    before = jnp.cumsum(picked, axis=0) - picked
    kept_rows = picked * (before < CAP).astype(jnp.int32)
    slot_ids = lax.broadcasted_iota(jnp.int32, (1, 1, CAP), 2)
    slot_marks = kept_rows[:, :, None] * (before[:, :, None] == slot_ids).astype(jnp.int32)
    marks_flat = slot_marks.reshape(tok_count, owners * CAP)
    selector = marks_flat.astype(jnp.bfloat16)
    outgoing = lax.dot_general(
        selector, tokens, (((0,), (0,)), ((), ())), preferred_element_type=jnp.float32
    ).astype(jnp.bfloat16)
    outgoing = outgoing.reshape(owners, CAP, model_width)
    gate_matrix = gate_weight[0]
    upper_matrix = up_weight[0]
    down_matrix = down_weight[0]
    arrived = lax.all_to_all(outgoing, "expert", split_axis=0, concat_axis=0, tiled=True)
    arrived, route_hit, route_weight, slot_marks = lax.optimization_barrier(
        (arrived, route_hit, route_weight, slot_marks)
    )
    item_count = arrived.shape[1]
    hidden, output = swiglu_rows(
        arrived.reshape(-1, model_width), gate_matrix, upper_matrix, down_matrix
    )
    results = output.reshape(owners, item_count, model_width)
    returned = lax.all_to_all(results, "expert", split_axis=0, concat_axis=0, tiled=True)
    returned_flat = returned.reshape(-1, model_width)
    owner_weight = jnp.sum(route_hit.astype(jnp.float32) * route_weight[:, :, None], axis=1)
    combine_matrix = (
        slot_marks.astype(jnp.float32) * owner_weight[:, :, None]
    ).reshape(tok_count, owners * CAP)
    weight_high, weight_low = split_bf16(combine_matrix)
    combined = combine_rows(weight_high, weight_low, returned_flat)
    hess_scale = 2.0 / (CAP * owners * pair_count)
    row_share = FF // pair_count
    pair_place = lax.axis_index("pair")
    hidden_wide = hidden.astype(jnp.float32)
    corner_part = lax.dot_general(
        hidden[:, :PANEL], hidden[:, :PANEL], (((0,), (0,)), ((), ())),
        preferred_element_type=jnp.float32,
    )
    square_part = jnp.broadcast_to(jnp.sum(hidden_wide * hidden_wide), (8, PANEL))
    pack = jnp.concatenate([corner_part, square_part], axis=0)
    pack_sum = pack
    for shift in range(1, pair_count):
        ring = [(i, (i + shift) % pair_count) for i in range(pair_count)]
        pack_sum = pack_sum + lax.ppermute(pack, "pair", ring)
    corner = pack_sum[:PANEL] * hess_scale
    damping = 0.01 * (pack_sum[PANEL, 0] * hess_scale) / FF
    lower_factor = jnp.linalg.cholesky(corner + damping * jnp.eye(PANEL, dtype=jnp.float32))
    gathered = [hidden]
    for shift in range(1, pair_count):
        ring = [(i, (i + shift) % pair_count) for i in range(pair_count)]
        gathered.append(lax.ppermute(hidden, "pair", ring))
    all_hidden = jnp.concatenate(gathered, axis=0)
    my_columns = lax.dynamic_slice_in_dim(all_hidden, pair_place * row_share, row_share, 1)
    my_rows = (
        lax.dot_general(
            my_columns, all_hidden, (((0,), (0,)), ((), ())), preferred_element_type=jnp.float32
        )
        * hess_scale
    )
    row_ids = pair_place * row_share + lax.broadcasted_iota(jnp.int32, (row_share, PANEL), 0)
    column_ids = lax.broadcasted_iota(jnp.int32, (row_share, PANEL), 1)
    leading = my_rows[:, :PANEL] + damping * (row_ids == column_ids).astype(jnp.float32)
    panel_rows = jax.scipy.linalg.solve_triangular(lower_factor, leading.T, lower=True).T
    return (combined, my_rows[None], panel_rows[None])


def solution(mesh):
    in_specs = (
        P(("expert", "pair"), None),
        P(("expert", "pair"), None),
        P(("expert", "pair"), None),
        P("expert", None, None),
        P("expert", None, None),
        P("expert", None, None),
    )
    out_specs = (P(("expert", "pair"), None), P("expert", "pair", None), P("expert", "pair", None))
    return jax.shard_map(
        per_device, mesh=mesh, in_specs=in_specs, out_specs=out_specs, check_vma=False
    )
```

```python
import jax
import jax.numpy as jnp
from jax import lax
from jax.sharding import PartitionSpec as P
from jax.experimental import pallas as pl
from jax.experimental.pallas import tpu as pltpu

EXPERTS = 128
FF = 768
PANEL = 128
CAP = 16


def swiglu_rows(flat_rows, gate_matrix, upper_matrix, down_matrix):
    gate_value = jnp.dot(flat_rows, gate_matrix, preferred_element_type=jnp.float32)
    upper_value = jnp.dot(flat_rows, upper_matrix, preferred_element_type=jnp.float32)
    hidden = (jax.nn.silu(gate_value) * upper_value).astype(jnp.bfloat16)
    output = jnp.dot(hidden, down_matrix, preferred_element_type=jnp.float32).astype(jnp.bfloat16)
    return (hidden, output)


def split_bf16(values):
    rounded = lax.reduce_precision(values, exponent_bits=8, mantissa_bits=7)
    return rounded.astype(jnp.bfloat16), (values - rounded).astype(jnp.bfloat16)


def combine_kernel(high_ref, low_ref, rows_ref, out_ref):
    rows = rows_ref[...]
    total = jnp.dot(high_ref[...], rows, preferred_element_type=jnp.float32)
    total = total + jnp.dot(low_ref[...], rows, preferred_element_type=jnp.float32)
    out_ref[...] = total.astype(out_ref.dtype)


def combine_rows(weight_high, weight_low, rows):
    tok_count, slot_count = weight_high.shape
    width = rows.shape[1]
    block = 2048
    return pl.pallas_call(
        combine_kernel,
        out_shape=jax.ShapeDtypeStruct((tok_count, width), jnp.bfloat16),
        grid=(width // block,),
        in_specs=[
            pl.BlockSpec((tok_count, slot_count), lambda j: (0, 0)),
            pl.BlockSpec((tok_count, slot_count), lambda j: (0, 0)),
            pl.BlockSpec((slot_count, block), lambda j: (0, j)),
        ],
        out_specs=pl.BlockSpec((tok_count, block), lambda j: (0, j)),
        cost_estimate=pl.CostEstimate(
            flops=4 * tok_count * slot_count * width,
            transcendentals=0,
            bytes_accessed=2 * (slot_count * width + tok_count * width + 2 * tok_count * slot_count),
        ),
    )(weight_high, weight_low, rows)


def per_device(tokens, expert_ids, route_weight, gate_weight, up_weight, down_weight):
    owners = lax.axis_size("expert")
    pair_count = lax.axis_size("pair")
    tok_count = tokens.shape[0]
    model_width = tokens.shape[1]
    per_owner = EXPERTS // owners
    in_flight = expert_ids % per_owner == 0
    owner_of = expert_ids // per_owner
    columns = lax.broadcasted_iota(jnp.int32, (1, 1, owners), 2)
    route_hit = (in_flight[:, :, None] & (owner_of[:, :, None] == columns)).astype(jnp.int32)
    picked = jnp.sum(route_hit, axis=1)
    before = jnp.cumsum(picked, axis=0) - picked
    rank_choice = jnp.sum(route_hit * before[:, None, :], axis=2)
    keep_choice = in_flight & (rank_choice < CAP)
    target = jnp.where(keep_choice, owner_of * CAP + rank_choice, -1)
    slot_iota = lax.broadcasted_iota(jnp.int32, (1, 1, owners * CAP), 2)
    hits = target[:, :, None] == slot_iota
    selector = jnp.any(hits, axis=1).astype(jnp.bfloat16)
    outgoing = lax.dot_general(
        selector, tokens, (((0,), (0,)), ((), ())), preferred_element_type=jnp.float32
    ).astype(jnp.bfloat16)
    outgoing = outgoing.reshape(owners, CAP, model_width)
    gate_matrix = gate_weight[0]
    upper_matrix = up_weight[0]
    down_matrix = down_weight[0]
    arrived = lax.all_to_all(outgoing, "expert", split_axis=0, concat_axis=0, tiled=True)
    item_count = arrived.shape[1]
    hidden, output = swiglu_rows(
        arrived.reshape(-1, model_width), gate_matrix, upper_matrix, down_matrix
    )
    results = output.reshape(owners, item_count, model_width)
    returned = lax.all_to_all(results, "expert", split_axis=0, concat_axis=0, tiled=True)
    returned_flat = returned.reshape(-1, model_width)
    combine_matrix = jnp.sum(jnp.where(hits, route_weight[:, :, None], 0.0), axis=1)
    weight_high, weight_low = split_bf16(combine_matrix)
    combined = combine_rows(weight_high, weight_low, returned_flat)
    hess_scale = 2.0 / (CAP * owners * pair_count)
    row_share = FF // pair_count
    pair_place = lax.axis_index("pair")
    hidden_wide = hidden.astype(jnp.float32)
    corner_part = lax.dot_general(
        hidden[:, :PANEL], hidden[:, :PANEL], (((0,), (0,)), ((), ())),
        preferred_element_type=jnp.float32,
    )
    square_part = jnp.broadcast_to(jnp.sum(hidden_wide * hidden_wide), (8, PANEL))
    pack = jnp.concatenate([corner_part, square_part], axis=0)
    pack_sum = pack
    for shift in range(1, pair_count):
        ring = [(i, (i + shift) % pair_count) for i in range(pair_count)]
        pack_sum = pack_sum + lax.ppermute(pack, "pair", ring)
    corner = pack_sum[:PANEL] * hess_scale
    damping = 0.01 * (pack_sum[PANEL, 0] * hess_scale) / FF
    lower_factor = jnp.linalg.cholesky(corner + damping * jnp.eye(PANEL, dtype=jnp.float32))
    gathered = [hidden]
    for shift in range(1, pair_count):
        ring = [(i, (i + shift) % pair_count) for i in range(pair_count)]
        gathered.append(lax.ppermute(hidden, "pair", ring))
    all_hidden = jnp.concatenate(gathered, axis=0)
    my_columns = lax.dynamic_slice_in_dim(all_hidden, pair_place * row_share, row_share, 1)
    my_rows = (
        lax.dot_general(
            my_columns, all_hidden, (((0,), (0,)), ((), ())), preferred_element_type=jnp.float32
        )
        * hess_scale
    )
    row_ids = pair_place * row_share + lax.broadcasted_iota(jnp.int32, (row_share, PANEL), 0)
    column_ids = lax.broadcasted_iota(jnp.int32, (row_share, PANEL), 1)
    leading = my_rows[:, :PANEL] + damping * (row_ids == column_ids).astype(jnp.float32)
    panel_rows = jax.scipy.linalg.solve_triangular(lower_factor, leading.T, lower=True).T
    return (combined, my_rows[None], panel_rows[None])


def solution(mesh):
    in_specs = (
        P(("expert", "pair"), None),
        P(("expert", "pair"), None),
        P(("expert", "pair"), None),
        P("expert", None, None),
        P("expert", None, None),
        P("expert", None, None),
    )
    out_specs = (P(("expert", "pair"), None), P("expert", "pair", None), P("expert", "pair", None))
    return jax.shard_map(
        per_device, mesh=mesh, in_specs=in_specs, out_specs=out_specs, check_vma=False
    )
```

```python
import jax
import jax.numpy as jnp
from jax import lax
from jax.sharding import PartitionSpec as P
from jax.experimental import pallas as pl
from jax.experimental.pallas import tpu as pltpu

EXPERTS = 128
FF = 768
PANEL = 128
CAP = 16


def swiglu_rows(flat_rows, gate_matrix, upper_matrix, down_matrix):
    gate_value = jnp.dot(flat_rows, gate_matrix, preferred_element_type=jnp.float32)
    upper_value = jnp.dot(flat_rows, upper_matrix, preferred_element_type=jnp.float32)
    hidden = (jax.nn.silu(gate_value) * upper_value).astype(jnp.bfloat16)
    output = jnp.dot(hidden, down_matrix, preferred_element_type=jnp.float32).astype(jnp.bfloat16)
    return (hidden, output)


def split_bf16(values):
    rounded = lax.reduce_precision(values, exponent_bits=8, mantissa_bits=7)
    return rounded.astype(jnp.bfloat16), (values - rounded).astype(jnp.bfloat16)


def combine_kernel(high_ref, low_ref, rows_ref, out_ref):
    rows = rows_ref[...]
    total = jnp.dot(high_ref[...], rows, preferred_element_type=jnp.float32)
    total = total + jnp.dot(low_ref[...], rows, preferred_element_type=jnp.float32)
    out_ref[...] = total.astype(out_ref.dtype)


def combine_rows(weight_high, weight_low, rows):
    tok_count, slot_count = weight_high.shape
    width = rows.shape[1]
    block = 2048
    return pl.pallas_call(
        combine_kernel,
        out_shape=jax.ShapeDtypeStruct((tok_count, width), jnp.bfloat16),
        grid=(width // block,),
        in_specs=[
            pl.BlockSpec((tok_count, slot_count), lambda j: (0, 0)),
            pl.BlockSpec((tok_count, slot_count), lambda j: (0, 0)),
            pl.BlockSpec((slot_count, block), lambda j: (0, j)),
        ],
        out_specs=pl.BlockSpec((tok_count, block), lambda j: (0, j)),
        cost_estimate=pl.CostEstimate(
            flops=4 * tok_count * slot_count * width,
            transcendentals=0,
            bytes_accessed=2 * (slot_count * width + tok_count * width + 2 * tok_count * slot_count),
        ),
    )(weight_high, weight_low, rows)


def route_kernel(ids_ref, tokens_ref, out_ref, target_ref):
    tok_count, choices = ids_ref.shape
    owners = out_ref.shape[0] // CAP
    per_owner = EXPERTS // owners
    ids = ids_ref[...]
    in_flight = (ids % per_owner) == 0
    owner_of = ids // per_owner
    owner_iota = lax.broadcasted_iota(jnp.int32, (tok_count, owners), 1)
    matches = []
    picked = jnp.zeros((tok_count, owners), jnp.float32)
    for k in range(choices):
        hit = (owner_of[:, k : k + 1] == owner_iota) & in_flight[:, k : k + 1]
        matches.append(hit)
        picked = picked + hit.astype(jnp.float32)
    row = lax.broadcasted_iota(jnp.int32, (tok_count, tok_count), 0)
    col = lax.broadcasted_iota(jnp.int32, (tok_count, tok_count), 1)
    earlier = (col < row).astype(jnp.bfloat16)
    before = jnp.dot(earlier, picked.astype(jnp.bfloat16), preferred_element_type=jnp.float32)
    slot_iota = lax.broadcasted_iota(jnp.int32, (tok_count, owners * CAP), 1)
    selector = jnp.zeros((tok_count, owners * CAP), jnp.float32)
    targets = []
    for k in range(choices):
        rank = jnp.sum(jnp.where(matches[k], before, 0.0), axis=1, keepdims=True).astype(jnp.int32)
        keep = in_flight[:, k : k + 1] & (rank < CAP)
        target = jnp.where(keep, owner_of[:, k : k + 1] * CAP + rank, -1)
        targets.append(target)
        selector = selector + (target == slot_iota).astype(jnp.float32)
    target_ref[...] = jnp.concatenate(targets, axis=1)
    chosen = selector.T.astype(jnp.bfloat16)
    width = tokens_ref.shape[1]
    block = 1024
    for c in range(width // block):
        part = jnp.dot(
            chosen, tokens_ref[:, c * block : (c + 1) * block], preferred_element_type=jnp.float32
        )
        out_ref[:, c * block : (c + 1) * block] = part.astype(out_ref.dtype)


def route_rows(expert_ids, tokens, owners):
    tok_count, choices = expert_ids.shape
    width = tokens.shape[1]
    slots = owners * CAP
    return pl.pallas_call(
        route_kernel,
        out_shape=(
            jax.ShapeDtypeStruct((slots, width), tokens.dtype),
            jax.ShapeDtypeStruct((tok_count, choices), jnp.int32),
        ),
        in_specs=[
            pl.BlockSpec(memory_space=pltpu.VMEM),
            pl.BlockSpec(memory_space=pltpu.VMEM),
        ],
        out_specs=(
            pl.BlockSpec(memory_space=pltpu.VMEM),
            pl.BlockSpec(memory_space=pltpu.VMEM),
        ),
        compiler_params=pltpu.CompilerParams(vmem_limit_bytes=48 * 1024 * 1024),
        cost_estimate=pl.CostEstimate(
            flops=2 * slots * tok_count * width,
            transcendentals=0,
            bytes_accessed=2 * (slots * width + tok_count * width),
        ),
    )(expert_ids, tokens)


def per_device(tokens, expert_ids, route_weight, gate_weight, up_weight, down_weight):
    owners = lax.axis_size("expert")
    pair_count = lax.axis_size("pair")
    tok_count = tokens.shape[0]
    model_width = tokens.shape[1]
    per_owner = EXPERTS // owners
    outgoing, target = route_rows(expert_ids, tokens, owners)
    outgoing = outgoing.reshape(owners, CAP, model_width)
    gate_matrix = gate_weight[0]
    upper_matrix = up_weight[0]
    down_matrix = down_weight[0]
    arrived = lax.all_to_all(outgoing, "expert", split_axis=0, concat_axis=0, tiled=True)
    item_count = arrived.shape[1]
    hidden, output = swiglu_rows(
        arrived.reshape(-1, model_width), gate_matrix, upper_matrix, down_matrix
    )
    results = output.reshape(owners, item_count, model_width)
    returned = lax.all_to_all(results, "expert", split_axis=0, concat_axis=0, tiled=True)
    returned_flat = returned.reshape(-1, model_width)
    slot_iota = lax.broadcasted_iota(jnp.int32, (1, 1, owners * CAP), 2)
    hits = target[:, :, None] == slot_iota
    combine_matrix = jnp.sum(jnp.where(hits, route_weight[:, :, None], 0.0), axis=1)
    weight_high, weight_low = split_bf16(combine_matrix)
    combined = combine_rows(weight_high, weight_low, returned_flat)
    hess_scale = 2.0 / (CAP * owners * pair_count)
    row_share = FF // pair_count
    pair_place = lax.axis_index("pair")
    hidden_wide = hidden.astype(jnp.float32)
    corner_part = lax.dot_general(
        hidden[:, :PANEL], hidden[:, :PANEL], (((0,), (0,)), ((), ())),
        preferred_element_type=jnp.float32,
    )
    square_part = jnp.broadcast_to(jnp.sum(hidden_wide * hidden_wide), (8, PANEL))
    pack = jnp.concatenate([corner_part, square_part], axis=0)
    pack_sum = pack
    for shift in range(1, pair_count):
        ring = [(i, (i + shift) % pair_count) for i in range(pair_count)]
        pack_sum = pack_sum + lax.ppermute(pack, "pair", ring)
    corner = pack_sum[:PANEL] * hess_scale
    damping = 0.01 * (pack_sum[PANEL, 0] * hess_scale) / FF
    lower_factor = jnp.linalg.cholesky(corner + damping * jnp.eye(PANEL, dtype=jnp.float32))
    gathered = [hidden]
    for shift in range(1, pair_count):
        ring = [(i, (i + shift) % pair_count) for i in range(pair_count)]
        gathered.append(lax.ppermute(hidden, "pair", ring))
    all_hidden = jnp.concatenate(gathered, axis=0)
    my_columns = lax.dynamic_slice_in_dim(all_hidden, pair_place * row_share, row_share, 1)
    my_rows = (
        lax.dot_general(
            my_columns, all_hidden, (((0,), (0,)), ((), ())), preferred_element_type=jnp.float32
        )
        * hess_scale
    )
    row_ids = pair_place * row_share + lax.broadcasted_iota(jnp.int32, (row_share, PANEL), 0)
    column_ids = lax.broadcasted_iota(jnp.int32, (row_share, PANEL), 1)
    leading = my_rows[:, :PANEL] + damping * (row_ids == column_ids).astype(jnp.float32)
    panel_rows = jax.scipy.linalg.solve_triangular(lower_factor, leading.T, lower=True).T
    return (combined, my_rows[None], panel_rows[None])


def solution(mesh):
    in_specs = (
        P(("expert", "pair"), None),
        P(("expert", "pair"), None),
        P(("expert", "pair"), None),
        P("expert", None, None),
        P("expert", None, None),
        P("expert", None, None),
    )
    out_specs = (P(("expert", "pair"), None), P("expert", "pair", None), P("expert", "pair", None))
    return jax.shard_map(
        per_device, mesh=mesh, in_specs=in_specs, out_specs=out_specs, check_vma=False
    )
```

```python
import jax
import jax.numpy as jnp
from jax import lax
from jax.sharding import PartitionSpec as P
from jax.experimental import pallas as pl
from jax.experimental.pallas import tpu as pltpu

EXPERTS = 128
FF = 768
PANEL = 128
CAP = 16


def swiglu_rows(flat_rows, gate_matrix, upper_matrix, down_matrix):
    gate_value = jnp.dot(flat_rows, gate_matrix, preferred_element_type=jnp.float32)
    upper_value = jnp.dot(flat_rows, upper_matrix, preferred_element_type=jnp.float32)
    hidden = (jax.nn.silu(gate_value) * upper_value).astype(jnp.bfloat16)
    output = jnp.dot(hidden, down_matrix, preferred_element_type=jnp.float32).astype(jnp.bfloat16)
    return (hidden, output)


def split_bf16(values):
    rounded = lax.reduce_precision(values, exponent_bits=8, mantissa_bits=7)
    return rounded.astype(jnp.bfloat16), (values - rounded).astype(jnp.bfloat16)


def combine_kernel(high_ref, low_ref, rows_ref, out_ref):
    rows = rows_ref[...]
    total = jnp.dot(high_ref[...], rows, preferred_element_type=jnp.float32)
    total = total + jnp.dot(low_ref[...], rows, preferred_element_type=jnp.float32)
    out_ref[...] = total.astype(out_ref.dtype)


def combine_rows(weight_high, weight_low, rows):
    tok_count, slot_count = weight_high.shape
    width = rows.shape[1]
    block = 2048
    return pl.pallas_call(
        combine_kernel,
        out_shape=jax.ShapeDtypeStruct((tok_count, width), jnp.bfloat16),
        grid=(width // block,),
        in_specs=[
            pl.BlockSpec((tok_count, slot_count), lambda j: (0, 0)),
            pl.BlockSpec((tok_count, slot_count), lambda j: (0, 0)),
            pl.BlockSpec((slot_count, block), lambda j: (0, j)),
        ],
        out_specs=pl.BlockSpec((tok_count, block), lambda j: (0, j)),
        cost_estimate=pl.CostEstimate(
            flops=4 * tok_count * slot_count * width,
            transcendentals=0,
            bytes_accessed=2 * (slot_count * width + tok_count * width + 2 * tok_count * slot_count),
        ),
    )(weight_high, weight_low, rows)


def route_kernel(ids_ref, tokens_hbm, out_ref, target_ref, tokens_vmem, copy_sem):
    fetch = pltpu.make_async_copy(tokens_hbm, tokens_vmem, copy_sem.at[0])
    fetch.start()
    choices, tok_count = ids_ref.shape
    slots = out_ref.shape[0]
    owners = slots // CAP
    per_owner = EXPERTS // owners
    ids = ids_ref[...]
    in_flight = (ids % per_owner) == 0
    owner_of = ids // per_owner
    owner_iota = lax.broadcasted_iota(jnp.int32, (owners, tok_count), 0)
    matches = []
    picked = jnp.zeros((owners, tok_count), jnp.float32)
    for k in range(choices):
        hit = (owner_of[k : k + 1, :] == owner_iota) & in_flight[k : k + 1, :]
        matches.append(hit)
        picked = picked + hit.astype(jnp.float32)
    row = lax.broadcasted_iota(jnp.int32, (tok_count, tok_count), 0)
    col = lax.broadcasted_iota(jnp.int32, (tok_count, tok_count), 1)
    later = (row < col).astype(jnp.bfloat16)
    before = jnp.dot(picked.astype(jnp.bfloat16), later, preferred_element_type=jnp.float32)
    slot_iota = lax.broadcasted_iota(jnp.int32, (slots, tok_count), 0)
    chosen = jnp.zeros((slots, tok_count), jnp.float32)
    targets = []
    for k in range(choices):
        rank = jnp.sum(jnp.where(matches[k], before, 0.0), axis=0, keepdims=True).astype(jnp.int32)
        keep = in_flight[k : k + 1, :] & (rank < CAP)
        target = jnp.where(keep, owner_of[k : k + 1, :] * CAP + rank, -1)
        targets.append(target)
        chosen = chosen + (target == slot_iota).astype(jnp.float32)
    target_ref[...] = jnp.concatenate(targets, axis=0)
    chosen = chosen.astype(jnp.bfloat16)
    fetch.wait()
    width = tokens_vmem.shape[1]
    block = 1024
    for c in range(width // block):
        part = jnp.dot(
            chosen, tokens_vmem[:, c * block : (c + 1) * block], preferred_element_type=jnp.float32
        )
        out_ref[:, c * block : (c + 1) * block] = part.astype(out_ref.dtype)


def route_rows(ids_by_choice, tokens, owners):
    choices, tok_count = ids_by_choice.shape
    width = tokens.shape[1]
    slots = owners * CAP
    return pl.pallas_call(
        route_kernel,
        out_shape=(
            jax.ShapeDtypeStruct((slots, width), tokens.dtype),
            jax.ShapeDtypeStruct((choices, tok_count), jnp.int32),
        ),
        in_specs=[
            pl.BlockSpec(memory_space=pltpu.VMEM),
            pl.BlockSpec(memory_space=pl.ANY),
        ],
        out_specs=(
            pl.BlockSpec(memory_space=pltpu.VMEM),
            pl.BlockSpec(memory_space=pltpu.VMEM),
        ),
        scratch_shapes=[
            pltpu.VMEM((tok_count, width), tokens.dtype),
            pltpu.SemaphoreType.DMA((1,)),
        ],
        compiler_params=pltpu.CompilerParams(vmem_limit_bytes=48 * 1024 * 1024),
        cost_estimate=pl.CostEstimate(
            flops=2 * slots * tok_count * width,
            transcendentals=0,
            bytes_accessed=2 * (slots * width + tok_count * width),
        ),
    )(ids_by_choice, tokens)


def per_device(tokens, expert_ids, route_weight, gate_weight, up_weight, down_weight):
    owners = lax.axis_size("expert")
    pair_count = lax.axis_size("pair")
    tok_count = tokens.shape[0]
    model_width = tokens.shape[1]
    per_owner = EXPERTS // owners
    outgoing, target_by_choice = route_rows(expert_ids.T, tokens, owners)
    target = target_by_choice.T
    outgoing = outgoing.reshape(owners, CAP, model_width)
    gate_matrix = gate_weight[0]
    upper_matrix = up_weight[0]
    down_matrix = down_weight[0]
    arrived = lax.all_to_all(outgoing, "expert", split_axis=0, concat_axis=0, tiled=True)
    item_count = arrived.shape[1]
    hidden, output = swiglu_rows(
        arrived.reshape(-1, model_width), gate_matrix, upper_matrix, down_matrix
    )
    results = output.reshape(owners, item_count, model_width)
    returned = lax.all_to_all(results, "expert", split_axis=0, concat_axis=0, tiled=True)
    returned_flat = returned.reshape(-1, model_width)
    slot_iota = lax.broadcasted_iota(jnp.int32, (1, 1, owners * CAP), 2)
    hits = target[:, :, None] == slot_iota
    combine_matrix = jnp.sum(jnp.where(hits, route_weight[:, :, None], 0.0), axis=1)
    weight_high, weight_low = split_bf16(combine_matrix)
    combined = combine_rows(weight_high, weight_low, returned_flat)
    hess_scale = 2.0 / (CAP * owners * pair_count)
    row_share = FF // pair_count
    pair_place = lax.axis_index("pair")
    hidden_wide = hidden.astype(jnp.float32)
    corner_part = lax.dot_general(
        hidden[:, :PANEL], hidden[:, :PANEL], (((0,), (0,)), ((), ())),
        preferred_element_type=jnp.float32,
    )
    square_part = jnp.broadcast_to(jnp.sum(hidden_wide * hidden_wide), (8, PANEL))
    pack = jnp.concatenate([corner_part, square_part], axis=0)
    pack_sum = pack
    for shift in range(1, pair_count):
        ring = [(i, (i + shift) % pair_count) for i in range(pair_count)]
        pack_sum = pack_sum + lax.ppermute(pack, "pair", ring)
    corner = pack_sum[:PANEL] * hess_scale
    damping = 0.01 * (pack_sum[PANEL, 0] * hess_scale) / FF
    lower_factor = jnp.linalg.cholesky(corner + damping * jnp.eye(PANEL, dtype=jnp.float32))
    gathered = [hidden]
    for shift in range(1, pair_count):
        ring = [(i, (i + shift) % pair_count) for i in range(pair_count)]
        gathered.append(lax.ppermute(hidden, "pair", ring))
    all_hidden = jnp.concatenate(gathered, axis=0)
    my_columns = lax.dynamic_slice_in_dim(all_hidden, pair_place * row_share, row_share, 1)
    my_rows = (
        lax.dot_general(
            my_columns, all_hidden, (((0,), (0,)), ((), ())), preferred_element_type=jnp.float32
        )
        * hess_scale
    )
    row_ids = pair_place * row_share + lax.broadcasted_iota(jnp.int32, (row_share, PANEL), 0)
    column_ids = lax.broadcasted_iota(jnp.int32, (row_share, PANEL), 1)
    leading = my_rows[:, :PANEL] + damping * (row_ids == column_ids).astype(jnp.float32)
    panel_rows = jax.scipy.linalg.solve_triangular(lower_factor, leading.T, lower=True).T
    return (combined, my_rows[None], panel_rows[None])


def solution(mesh):
    in_specs = (
        P(("expert", "pair"), None),
        P(("expert", "pair"), None),
        P(("expert", "pair"), None),
        P("expert", None, None),
        P("expert", None, None),
        P("expert", None, None),
    )
    out_specs = (P(("expert", "pair"), None), P("expert", "pair", None), P("expert", "pair", None))
    return jax.shard_map(
        per_device, mesh=mesh, in_specs=in_specs, out_specs=out_specs, check_vma=False
    )
```

```python
import jax
import jax.numpy as jnp
from jax import lax
from jax.sharding import PartitionSpec as P
from jax.experimental import pallas as pl
from jax.experimental.pallas import tpu as pltpu

EXPERTS = 128
FF = 768
PANEL = 128
CAP = 16


def swiglu_rows(flat_rows, gate_matrix, upper_matrix, down_matrix):
    gate_value = jnp.dot(flat_rows, gate_matrix, preferred_element_type=jnp.float32)
    upper_value = jnp.dot(flat_rows, upper_matrix, preferred_element_type=jnp.float32)
    hidden = (jax.nn.silu(gate_value) * upper_value).astype(jnp.bfloat16)
    output = jnp.dot(hidden, down_matrix, preferred_element_type=jnp.float32).astype(jnp.bfloat16)
    return (hidden, output)


def split_bf16(values):
    rounded = lax.reduce_precision(values, exponent_bits=8, mantissa_bits=7)
    return rounded.astype(jnp.bfloat16), (values - rounded).astype(jnp.bfloat16)


def combine_kernel(high_ref, low_ref, rows_ref, out_ref):
    rows = rows_ref[...]
    total = jnp.dot(high_ref[...], rows, preferred_element_type=jnp.float32)
    total = total + jnp.dot(low_ref[...], rows, preferred_element_type=jnp.float32)
    out_ref[...] = total.astype(out_ref.dtype)


def combine_rows(weight_high, weight_low, rows):
    tok_count, slot_count = weight_high.shape
    width = rows.shape[1]
    block = 2048
    return pl.pallas_call(
        combine_kernel,
        out_shape=jax.ShapeDtypeStruct((tok_count, width), jnp.bfloat16),
        grid=(width // block,),
        in_specs=[
            pl.BlockSpec((tok_count, slot_count), lambda j: (0, 0)),
            pl.BlockSpec((tok_count, slot_count), lambda j: (0, 0)),
            pl.BlockSpec((slot_count, block), lambda j: (0, j)),
        ],
        out_specs=pl.BlockSpec((tok_count, block), lambda j: (0, j)),
        cost_estimate=pl.CostEstimate(
            flops=4 * tok_count * slot_count * width,
            transcendentals=0,
            bytes_accessed=2 * (slot_count * width + tok_count * width + 2 * tok_count * slot_count),
        ),
    )(weight_high, weight_low, rows)


def route_kernel(ids_hbm, tokens_hbm, out_ref, target_ref, ids_ref, tokens_vmem, copy_sem):
    fetch_ids = pltpu.make_async_copy(ids_hbm, ids_ref, copy_sem.at[1])
    fetch_ids.start()
    fetch = pltpu.make_async_copy(tokens_hbm, tokens_vmem, copy_sem.at[0])
    fetch.start()
    fetch_ids.wait()
    choices, tok_count = ids_ref.shape
    slots = out_ref.shape[0]
    owners = slots // CAP
    per_owner = EXPERTS // owners
    ids = ids_ref[...]
    in_flight = (ids % per_owner) == 0
    owner_of = ids // per_owner
    owner_iota = lax.broadcasted_iota(jnp.int32, (owners, tok_count), 0)
    matches = []
    picked = jnp.zeros((owners, tok_count), jnp.float32)
    for k in range(choices):
        hit = (owner_of[k : k + 1, :] == owner_iota) & in_flight[k : k + 1, :]
        matches.append(hit)
        picked = picked + hit.astype(jnp.float32)
    row = lax.broadcasted_iota(jnp.int32, (tok_count, tok_count), 0)
    col = lax.broadcasted_iota(jnp.int32, (tok_count, tok_count), 1)
    later = (row < col).astype(jnp.bfloat16)
    before = jnp.dot(picked.astype(jnp.bfloat16), later, preferred_element_type=jnp.float32)
    slot_iota = lax.broadcasted_iota(jnp.int32, (slots, tok_count), 0)
    chosen = jnp.zeros((slots, tok_count), jnp.float32)
    targets = []
    for k in range(choices):
        rank = jnp.sum(jnp.where(matches[k], before, 0.0), axis=0, keepdims=True).astype(jnp.int32)
        keep = in_flight[k : k + 1, :] & (rank < CAP)
        target = jnp.where(keep, owner_of[k : k + 1, :] * CAP + rank, -1)
        targets.append(target)
        chosen = chosen + (target == slot_iota).astype(jnp.float32)
    target_ref[...] = jnp.concatenate(targets, axis=0)
    chosen = chosen.astype(jnp.bfloat16)
    fetch.wait()
    width = tokens_vmem.shape[1]
    block = 1024
    for c in range(width // block):
        part = jnp.dot(
            chosen, tokens_vmem[:, c * block : (c + 1) * block], preferred_element_type=jnp.float32
        )
        out_ref[:, c * block : (c + 1) * block] = part.astype(out_ref.dtype)


def route_rows(ids_by_choice, tokens, owners):
    choices, tok_count = ids_by_choice.shape
    width = tokens.shape[1]
    slots = owners * CAP
    return pl.pallas_call(
        route_kernel,
        out_shape=(
            jax.ShapeDtypeStruct((slots, width), tokens.dtype),
            jax.ShapeDtypeStruct((choices, tok_count), jnp.int32),
        ),
        in_specs=[
            pl.BlockSpec(memory_space=pl.ANY),
            pl.BlockSpec(memory_space=pl.ANY),
        ],
        out_specs=(
            pl.BlockSpec(memory_space=pltpu.VMEM),
            pl.BlockSpec(memory_space=pltpu.VMEM),
        ),
        scratch_shapes=[
            pltpu.VMEM((choices, tok_count), jnp.int32),
            pltpu.VMEM((tok_count, width), tokens.dtype),
            pltpu.SemaphoreType.DMA((2,)),
        ],
        cost_estimate=pl.CostEstimate(
            flops=2 * slots * tok_count * width,
            transcendentals=0,
            bytes_accessed=2 * (slots * width + tok_count * width),
        ),
    )(ids_by_choice, tokens)


def per_device(tokens, expert_ids, route_weight, gate_weight, up_weight, down_weight):
    owners = lax.axis_size("expert")
    pair_count = lax.axis_size("pair")
    tok_count = tokens.shape[0]
    model_width = tokens.shape[1]
    per_owner = EXPERTS // owners
    outgoing, target_by_choice = route_rows(expert_ids.T, tokens, owners)
    target = target_by_choice.T
    outgoing = outgoing.reshape(owners, CAP, model_width)
    gate_matrix = gate_weight[0]
    upper_matrix = up_weight[0]
    down_matrix = down_weight[0]
    arrived = lax.all_to_all(outgoing, "expert", split_axis=0, concat_axis=0, tiled=True)
    item_count = arrived.shape[1]
    hidden, output = swiglu_rows(
        arrived.reshape(-1, model_width), gate_matrix, upper_matrix, down_matrix
    )
    results = output.reshape(owners, item_count, model_width)
    returned = lax.all_to_all(results, "expert", split_axis=0, concat_axis=0, tiled=True)
    returned_flat = returned.reshape(-1, model_width)
    slot_iota = lax.broadcasted_iota(jnp.int32, (1, 1, owners * CAP), 2)
    hits = target[:, :, None] == slot_iota
    combine_matrix = jnp.sum(jnp.where(hits, route_weight[:, :, None], 0.0), axis=1)
    weight_high, weight_low = split_bf16(combine_matrix)
    combined = combine_rows(weight_high, weight_low, returned_flat)
    hess_scale = 2.0 / (CAP * owners * pair_count)
    row_share = FF // pair_count
    pair_place = lax.axis_index("pair")
    hidden_wide = hidden.astype(jnp.float32)
    corner_part = lax.dot_general(
        hidden[:, :PANEL], hidden[:, :PANEL], (((0,), (0,)), ((), ())),
        preferred_element_type=jnp.float32,
    )
    square_part = jnp.broadcast_to(jnp.sum(hidden_wide * hidden_wide), (8, PANEL))
    pack = jnp.concatenate([corner_part, square_part], axis=0)
    pack_sum = pack
    for shift in range(1, pair_count):
        ring = [(i, (i + shift) % pair_count) for i in range(pair_count)]
        pack_sum = pack_sum + lax.ppermute(pack, "pair", ring)
    corner = pack_sum[:PANEL] * hess_scale
    damping = 0.01 * (pack_sum[PANEL, 0] * hess_scale) / FF
    lower_factor = jnp.linalg.cholesky(corner + damping * jnp.eye(PANEL, dtype=jnp.float32))
    gathered = [hidden]
    for shift in range(1, pair_count):
        ring = [(i, (i + shift) % pair_count) for i in range(pair_count)]
        gathered.append(lax.ppermute(hidden, "pair", ring))
    all_hidden = jnp.concatenate(gathered, axis=0)
    my_columns = lax.dynamic_slice_in_dim(all_hidden, pair_place * row_share, row_share, 1)
    my_rows = (
        lax.dot_general(
            my_columns, all_hidden, (((0,), (0,)), ((), ())), preferred_element_type=jnp.float32
        )
        * hess_scale
    )
    row_ids = pair_place * row_share + lax.broadcasted_iota(jnp.int32, (row_share, PANEL), 0)
    column_ids = lax.broadcasted_iota(jnp.int32, (row_share, PANEL), 1)
    leading = my_rows[:, :PANEL] + damping * (row_ids == column_ids).astype(jnp.float32)
    panel_rows = jax.scipy.linalg.solve_triangular(lower_factor, leading.T, lower=True).T
    return (combined, my_rows[None], panel_rows[None])


def solution(mesh):
    in_specs = (
        P(("expert", "pair"), None),
        P(("expert", "pair"), None),
        P(("expert", "pair"), None),
        P("expert", None, None),
        P("expert", None, None),
        P("expert", None, None),
    )
    out_specs = (P(("expert", "pair"), None), P("expert", "pair", None), P("expert", "pair", None))
    return jax.shard_map(
        per_device, mesh=mesh, in_specs=in_specs, out_specs=out_specs, check_vma=False
    )
```

```python
import jax
import jax.numpy as jnp
from jax import lax
from jax.sharding import PartitionSpec as P
from jax.experimental import pallas as pl
from jax.experimental.pallas import tpu as pltpu

EXPERTS = 128
FF = 768
PANEL = 128
CAP = 16


def swiglu_rows(flat_rows, gate_matrix, upper_matrix, down_matrix):
    gate_value = jnp.dot(flat_rows, gate_matrix, preferred_element_type=jnp.float32)
    upper_value = jnp.dot(flat_rows, upper_matrix, preferred_element_type=jnp.float32)
    hidden = (jax.nn.silu(gate_value) * upper_value).astype(jnp.bfloat16)
    output = jnp.dot(hidden, down_matrix, preferred_element_type=jnp.float32).astype(jnp.bfloat16)
    return (hidden, output)


def split_bf16(values):
    rounded = lax.reduce_precision(values, exponent_bits=8, mantissa_bits=7)
    return rounded.astype(jnp.bfloat16), (values - rounded).astype(jnp.bfloat16)


def combine_kernel(high_ref, low_ref, rows_ref, out_ref):
    rows = rows_ref[...]
    total = jnp.dot(high_ref[...], rows, preferred_element_type=jnp.float32)
    total = total + jnp.dot(low_ref[...], rows, preferred_element_type=jnp.float32)
    out_ref[...] = total.astype(out_ref.dtype)


def combine_rows(weight_high, weight_low, rows):
    tok_count, slot_count = weight_high.shape
    width = rows.shape[1]
    block = 2048
    return pl.pallas_call(
        combine_kernel,
        out_shape=jax.ShapeDtypeStruct((tok_count, width), jnp.bfloat16),
        grid=(width // block,),
        in_specs=[
            pl.BlockSpec((tok_count, slot_count), lambda j: (0, 0)),
            pl.BlockSpec((tok_count, slot_count), lambda j: (0, 0)),
            pl.BlockSpec((slot_count, block), lambda j: (0, j)),
        ],
        out_specs=pl.BlockSpec((tok_count, block), lambda j: (0, j)),
        cost_estimate=pl.CostEstimate(
            flops=4 * tok_count * slot_count * width,
            transcendentals=0,
            bytes_accessed=2 * (slot_count * width + tok_count * width + 2 * tok_count * slot_count),
        ),
    )(weight_high, weight_low, rows)


def route_kernel(ids_ref, chosen_ref, target_ref):
    choices, tok_count = ids_ref.shape
    slots = chosen_ref.shape[0]
    owners = slots // CAP
    per_owner = EXPERTS // owners
    ids = ids_ref[...]
    in_flight = (ids % per_owner) == 0
    owner_of = ids // per_owner
    owner_iota = lax.broadcasted_iota(jnp.int32, (owners, tok_count), 0)
    matches = []
    picked = jnp.zeros((owners, tok_count), jnp.float32)
    for k in range(choices):
        hit = (owner_of[k : k + 1, :] == owner_iota) & in_flight[k : k + 1, :]
        matches.append(hit)
        picked = picked + hit.astype(jnp.float32)
    row = lax.broadcasted_iota(jnp.int32, (tok_count, tok_count), 0)
    col = lax.broadcasted_iota(jnp.int32, (tok_count, tok_count), 1)
    later = (row < col).astype(jnp.bfloat16)
    before = jnp.dot(picked.astype(jnp.bfloat16), later, preferred_element_type=jnp.float32)
    slot_iota = lax.broadcasted_iota(jnp.int32, (slots, tok_count), 0)
    chosen = jnp.zeros((slots, tok_count), jnp.float32)
    targets = []
    for k in range(choices):
        rank = jnp.sum(jnp.where(matches[k], before, 0.0), axis=0, keepdims=True).astype(jnp.int32)
        keep = in_flight[k : k + 1, :] & (rank < CAP)
        target = jnp.where(keep, owner_of[k : k + 1, :] * CAP + rank, -1)
        targets.append(target)
        chosen = chosen + (target == slot_iota).astype(jnp.float32)
    target_ref[...] = jnp.concatenate(targets, axis=0)
    chosen_ref[...] = chosen.astype(chosen_ref.dtype)


def route_rows(ids_by_choice, tokens, owners):
    choices, tok_count = ids_by_choice.shape
    slots = owners * CAP
    chosen, target = pl.pallas_call(
        route_kernel,
        out_shape=(
            jax.ShapeDtypeStruct((slots, tok_count), jnp.bfloat16),
            jax.ShapeDtypeStruct((choices, tok_count), jnp.int32),
        ),
        in_specs=[pl.BlockSpec(memory_space=pltpu.VMEM)],
        out_specs=(
            pl.BlockSpec(memory_space=pltpu.VMEM),
            pl.BlockSpec(memory_space=pltpu.VMEM),
        ),
        cost_estimate=pl.CostEstimate(
            flops=2 * owners * tok_count * tok_count, transcendentals=0, bytes_accessed=4 * slots * tok_count
        ),
    )(ids_by_choice)
    outgoing = jnp.dot(chosen, tokens, preferred_element_type=jnp.float32).astype(tokens.dtype)
    return outgoing, target


def per_device(tokens, expert_ids, route_weight, gate_weight, up_weight, down_weight):
    owners = lax.axis_size("expert")
    pair_count = lax.axis_size("pair")
    tok_count = tokens.shape[0]
    model_width = tokens.shape[1]
    per_owner = EXPERTS // owners
    outgoing, target_by_choice = route_rows(expert_ids.T, tokens, owners)
    target = target_by_choice.T
    outgoing = outgoing.reshape(owners, CAP, model_width)
    gate_matrix = gate_weight[0]
    upper_matrix = up_weight[0]
    down_matrix = down_weight[0]
    arrived = lax.all_to_all(outgoing, "expert", split_axis=0, concat_axis=0, tiled=True)
    item_count = arrived.shape[1]
    hidden, output = swiglu_rows(
        arrived.reshape(-1, model_width), gate_matrix, upper_matrix, down_matrix
    )
    results = output.reshape(owners, item_count, model_width)
    returned = lax.all_to_all(results, "expert", split_axis=0, concat_axis=0, tiled=True)
    returned_flat = returned.reshape(-1, model_width)
    slot_iota = lax.broadcasted_iota(jnp.int32, (1, 1, owners * CAP), 2)
    hits = target[:, :, None] == slot_iota
    combine_matrix = jnp.sum(jnp.where(hits, route_weight[:, :, None], 0.0), axis=1)
    weight_high, weight_low = split_bf16(combine_matrix)
    combined = combine_rows(weight_high, weight_low, returned_flat)
    hess_scale = 2.0 / (CAP * owners * pair_count)
    row_share = FF // pair_count
    pair_place = lax.axis_index("pair")
    hidden_wide = hidden.astype(jnp.float32)
    corner_part = lax.dot_general(
        hidden[:, :PANEL], hidden[:, :PANEL], (((0,), (0,)), ((), ())),
        preferred_element_type=jnp.float32,
    )
    square_part = jnp.broadcast_to(jnp.sum(hidden_wide * hidden_wide), (8, PANEL))
    pack = jnp.concatenate([corner_part, square_part], axis=0)
    pack_sum = pack
    for shift in range(1, pair_count):
        ring = [(i, (i + shift) % pair_count) for i in range(pair_count)]
        pack_sum = pack_sum + lax.ppermute(pack, "pair", ring)
    corner = pack_sum[:PANEL] * hess_scale
    damping = 0.01 * (pack_sum[PANEL, 0] * hess_scale) / FF
    lower_factor = jnp.linalg.cholesky(corner + damping * jnp.eye(PANEL, dtype=jnp.float32))
    gathered = [hidden]
    for shift in range(1, pair_count):
        ring = [(i, (i + shift) % pair_count) for i in range(pair_count)]
        gathered.append(lax.ppermute(hidden, "pair", ring))
    all_hidden = jnp.concatenate(gathered, axis=0)
    my_columns = lax.dynamic_slice_in_dim(all_hidden, pair_place * row_share, row_share, 1)
    my_rows = (
        lax.dot_general(
            my_columns, all_hidden, (((0,), (0,)), ((), ())), preferred_element_type=jnp.float32
        )
        * hess_scale
    )
    row_ids = pair_place * row_share + lax.broadcasted_iota(jnp.int32, (row_share, PANEL), 0)
    column_ids = lax.broadcasted_iota(jnp.int32, (row_share, PANEL), 1)
    leading = my_rows[:, :PANEL] + damping * (row_ids == column_ids).astype(jnp.float32)
    panel_rows = jax.scipy.linalg.solve_triangular(lower_factor, leading.T, lower=True).T
    return (combined, my_rows[None], panel_rows[None])


def solution(mesh):
    in_specs = (
        P(("expert", "pair"), None),
        P(("expert", "pair"), None),
        P(("expert", "pair"), None),
        P("expert", None, None),
        P("expert", None, None),
        P("expert", None, None),
    )
    out_specs = (P(("expert", "pair"), None), P("expert", "pair", None), P("expert", "pair", None))
    return jax.shard_map(
        per_device, mesh=mesh, in_specs=in_specs, out_specs=out_specs, check_vma=False
    )
```

```python
import jax
import jax.numpy as jnp
from jax import lax
from jax.sharding import PartitionSpec as P
from jax.experimental import pallas as pl
from jax.experimental.pallas import tpu as pltpu

EXPERTS = 128
FF = 768
PANEL = 128
CAP = 16


def swiglu_rows(flat_rows, gate_matrix, upper_matrix, down_matrix):
    gate_value = jnp.dot(flat_rows, gate_matrix, preferred_element_type=jnp.float32)
    upper_value = jnp.dot(flat_rows, upper_matrix, preferred_element_type=jnp.float32)
    hidden = (jax.nn.silu(gate_value) * upper_value).astype(jnp.bfloat16)
    output = jnp.dot(hidden, down_matrix, preferred_element_type=jnp.float32).astype(jnp.bfloat16)
    return (hidden, output)


def split_bf16(values):
    rounded = lax.reduce_precision(values, exponent_bits=8, mantissa_bits=7)
    return rounded.astype(jnp.bfloat16), (values - rounded).astype(jnp.bfloat16)


def combine_kernel(high_ref, low_ref, rows_ref, out_ref):
    rows = rows_ref[...]
    total = jnp.dot(high_ref[...], rows, preferred_element_type=jnp.float32)
    total = total + jnp.dot(low_ref[...], rows, preferred_element_type=jnp.float32)
    out_ref[...] = total.astype(out_ref.dtype)


def combine_rows(weight_high, weight_low, rows):
    tok_count, slot_count = weight_high.shape
    width = rows.shape[1]
    block = 2048
    return pl.pallas_call(
        combine_kernel,
        out_shape=jax.ShapeDtypeStruct((tok_count, width), jnp.bfloat16),
        grid=(width // block,),
        in_specs=[
            pl.BlockSpec((tok_count, slot_count), lambda j: (0, 0)),
            pl.BlockSpec((tok_count, slot_count), lambda j: (0, 0)),
            pl.BlockSpec((slot_count, block), lambda j: (0, j)),
        ],
        out_specs=pl.BlockSpec((tok_count, block), lambda j: (0, j)),
        cost_estimate=pl.CostEstimate(
            flops=4 * tok_count * slot_count * width,
            transcendentals=0,
            bytes_accessed=2 * (slot_count * width + tok_count * width + 2 * tok_count * slot_count),
        ),
    )(weight_high, weight_low, rows)


def route_kernel(ids_ref, tokens_hbm, out_ref, target_ref, tokens_vmem, copy_sem):
    fetch = pltpu.make_async_copy(tokens_hbm, tokens_vmem, copy_sem.at[0])
    fetch.start()
    choices, tok_count = ids_ref.shape
    slots = out_ref.shape[0]
    owners = slots // CAP
    per_owner = EXPERTS // owners
    ids = ids_ref[...]
    in_flight = (ids % per_owner) == 0
    owner_of = ids // per_owner
    owner_iota = lax.broadcasted_iota(jnp.int32, (owners, tok_count), 0)
    matches = []
    picked = jnp.zeros((owners, tok_count), jnp.float32)
    for k in range(choices):
        hit = (owner_of[k : k + 1, :] == owner_iota) & in_flight[k : k + 1, :]
        matches.append(hit)
        picked = picked + hit.astype(jnp.float32)
    row = lax.broadcasted_iota(jnp.int32, (tok_count, tok_count), 0)
    col = lax.broadcasted_iota(jnp.int32, (tok_count, tok_count), 1)
    later = (row < col).astype(jnp.bfloat16)
    before = jnp.dot(picked.astype(jnp.bfloat16), later, preferred_element_type=jnp.float32)
    targets = []
    for k in range(choices):
        rank = jnp.sum(jnp.where(matches[k], before, 0.0), axis=0, keepdims=True).astype(jnp.int32)
        keep = in_flight[k : k + 1, :] & (rank < CAP)
        target = jnp.where(keep, owner_of[k : k + 1, :] * CAP + rank, -1)
        targets.append(target)
    target_ref[...] = jnp.concatenate(targets, axis=0)
    owner_rank = jnp.where((picked > 0.0) & (before < CAP), before, -1.0)
    slot_iota = lax.broadcasted_iota(jnp.int32, (owners, CAP, tok_count), 1).astype(jnp.float32)
    chosen = (owner_rank[:, None, :] == slot_iota).astype(jnp.float32)
    chosen = chosen.reshape(slots, tok_count).astype(jnp.bfloat16)
    fetch.wait()
    width = tokens_vmem.shape[1]
    block = 1024
    for c in range(width // block):
        part = jnp.dot(
            chosen, tokens_vmem[:, c * block : (c + 1) * block], preferred_element_type=jnp.float32
        )
        out_ref[:, c * block : (c + 1) * block] = part.astype(out_ref.dtype)


def route_rows(ids_by_choice, tokens, owners):
    choices, tok_count = ids_by_choice.shape
    width = tokens.shape[1]
    slots = owners * CAP
    return pl.pallas_call(
        route_kernel,
        out_shape=(
            jax.ShapeDtypeStruct((slots, width), tokens.dtype),
            jax.ShapeDtypeStruct((choices, tok_count), jnp.int32),
        ),
        in_specs=[
            pl.BlockSpec(memory_space=pltpu.VMEM),
            pl.BlockSpec(memory_space=pl.ANY),
        ],
        out_specs=(
            pl.BlockSpec(memory_space=pltpu.VMEM),
            pl.BlockSpec(memory_space=pltpu.VMEM),
        ),
        scratch_shapes=[
            pltpu.VMEM((tok_count, width), tokens.dtype),
            pltpu.SemaphoreType.DMA((1,)),
        ],
        compiler_params=pltpu.CompilerParams(vmem_limit_bytes=48 * 1024 * 1024),
        cost_estimate=pl.CostEstimate(
            flops=2 * slots * tok_count * width,
            transcendentals=0,
            bytes_accessed=2 * (slots * width + tok_count * width),
        ),
    )(ids_by_choice, tokens)


def per_device(tokens, expert_ids, route_weight, gate_weight, up_weight, down_weight):
    owners = lax.axis_size("expert")
    pair_count = lax.axis_size("pair")
    tok_count = tokens.shape[0]
    model_width = tokens.shape[1]
    per_owner = EXPERTS // owners
    outgoing, target_by_choice = route_rows(expert_ids.T, tokens, owners)
    target = target_by_choice.T
    outgoing = outgoing.reshape(owners, CAP, model_width)
    gate_matrix = gate_weight[0]
    upper_matrix = up_weight[0]
    down_matrix = down_weight[0]
    arrived = lax.all_to_all(outgoing, "expert", split_axis=0, concat_axis=0, tiled=True)
    item_count = arrived.shape[1]
    hidden, output = swiglu_rows(
        arrived.reshape(-1, model_width), gate_matrix, upper_matrix, down_matrix
    )
    results = output.reshape(owners, item_count, model_width)
    returned = lax.all_to_all(results, "expert", split_axis=0, concat_axis=0, tiled=True)
    returned_flat = returned.reshape(-1, model_width)
    slot_iota = lax.broadcasted_iota(jnp.int32, (1, 1, owners * CAP), 2)
    hits = target[:, :, None] == slot_iota
    combine_matrix = jnp.sum(jnp.where(hits, route_weight[:, :, None], 0.0), axis=1)
    weight_high, weight_low = split_bf16(combine_matrix)
    combined = combine_rows(weight_high, weight_low, returned_flat)
    hess_scale = 2.0 / (CAP * owners * pair_count)
    row_share = FF // pair_count
    pair_place = lax.axis_index("pair")
    hidden_wide = hidden.astype(jnp.float32)
    corner_part = lax.dot_general(
        hidden[:, :PANEL], hidden[:, :PANEL], (((0,), (0,)), ((), ())),
        preferred_element_type=jnp.float32,
    )
    square_part = jnp.broadcast_to(jnp.sum(hidden_wide * hidden_wide), (8, PANEL))
    pack = jnp.concatenate([corner_part, square_part], axis=0)
    pack_sum = pack
    for shift in range(1, pair_count):
        ring = [(i, (i + shift) % pair_count) for i in range(pair_count)]
        pack_sum = pack_sum + lax.ppermute(pack, "pair", ring)
    corner = pack_sum[:PANEL] * hess_scale
    damping = 0.01 * (pack_sum[PANEL, 0] * hess_scale) / FF
    lower_factor = jnp.linalg.cholesky(corner + damping * jnp.eye(PANEL, dtype=jnp.float32))
    gathered = [hidden]
    for shift in range(1, pair_count):
        ring = [(i, (i + shift) % pair_count) for i in range(pair_count)]
        gathered.append(lax.ppermute(hidden, "pair", ring))
    all_hidden = jnp.concatenate(gathered, axis=0)
    my_columns = lax.dynamic_slice_in_dim(all_hidden, pair_place * row_share, row_share, 1)
    my_rows = (
        lax.dot_general(
            my_columns, all_hidden, (((0,), (0,)), ((), ())), preferred_element_type=jnp.float32
        )
        * hess_scale
    )
    row_ids = pair_place * row_share + lax.broadcasted_iota(jnp.int32, (row_share, PANEL), 0)
    column_ids = lax.broadcasted_iota(jnp.int32, (row_share, PANEL), 1)
    leading = my_rows[:, :PANEL] + damping * (row_ids == column_ids).astype(jnp.float32)
    panel_rows = jax.scipy.linalg.solve_triangular(lower_factor, leading.T, lower=True).T
    return (combined, my_rows[None], panel_rows[None])


def solution(mesh):
    in_specs = (
        P(("expert", "pair"), None),
        P(("expert", "pair"), None),
        P(("expert", "pair"), None),
        P("expert", None, None),
        P("expert", None, None),
        P("expert", None, None),
    )
    out_specs = (P(("expert", "pair"), None), P("expert", "pair", None), P("expert", "pair", None))
    return jax.shard_map(
        per_device, mesh=mesh, in_specs=in_specs, out_specs=out_specs, check_vma=False
    )
```

```python
import jax
import jax.numpy as jnp
from jax import lax
from jax.sharding import PartitionSpec as P
from jax.experimental import pallas as pl
from jax.experimental.pallas import tpu as pltpu

EXPERTS = 128
FF = 768
PANEL = 128
CAP = 16


def swiglu_rows(flat_rows, gate_matrix, upper_matrix, down_matrix):
    gate_value = jnp.dot(flat_rows, gate_matrix, preferred_element_type=jnp.float32)
    upper_value = jnp.dot(flat_rows, upper_matrix, preferred_element_type=jnp.float32)
    hidden = (jax.nn.silu(gate_value) * upper_value).astype(jnp.bfloat16)
    output = jnp.dot(hidden, down_matrix, preferred_element_type=jnp.float32).astype(jnp.bfloat16)
    return (hidden, output)


def split_bf16(values):
    rounded = lax.reduce_precision(values, exponent_bits=8, mantissa_bits=7)
    return rounded.astype(jnp.bfloat16), (values - rounded).astype(jnp.bfloat16)


def combine_kernel(high_ref, low_ref, rows_ref, out_ref):
    rows = rows_ref[...]
    total = jnp.dot(high_ref[...], rows, preferred_element_type=jnp.float32)
    total = total + jnp.dot(low_ref[...], rows, preferred_element_type=jnp.float32)
    out_ref[...] = total.astype(out_ref.dtype)


def combine_rows(weight_high, weight_low, rows):
    tok_count, slot_count = weight_high.shape
    width = rows.shape[1]
    block = 2048
    return pl.pallas_call(
        combine_kernel,
        out_shape=jax.ShapeDtypeStruct((tok_count, width), jnp.bfloat16),
        grid=(width // block,),
        in_specs=[
            pl.BlockSpec((tok_count, slot_count), lambda j: (0, 0)),
            pl.BlockSpec((tok_count, slot_count), lambda j: (0, 0)),
            pl.BlockSpec((slot_count, block), lambda j: (0, j)),
        ],
        out_specs=pl.BlockSpec((tok_count, block), lambda j: (0, j)),
        cost_estimate=pl.CostEstimate(
            flops=4 * tok_count * slot_count * width,
            transcendentals=0,
            bytes_accessed=2 * (slot_count * width + tok_count * width + 2 * tok_count * slot_count),
        ),
    )(weight_high, weight_low, rows)


def route_kernel(ids_ref, tokens_hbm, out_ref, target_ref, tokens_vmem, copy_sem):
    fetch = pltpu.make_async_copy(tokens_hbm, tokens_vmem, copy_sem.at[0])
    fetch.start()
    choices, tok_count = ids_ref.shape
    slots = out_ref.shape[0]
    owners = slots // CAP
    per_owner = EXPERTS // owners
    ids = ids_ref[...]
    in_flight = (ids % per_owner) == 0
    owner_of = ids // per_owner
    owner_iota = lax.broadcasted_iota(jnp.int32, (owners, tok_count), 0)
    matches = []
    picked = jnp.zeros((owners, tok_count), jnp.float32)
    for k in range(choices):
        hit = (owner_of[k : k + 1, :] == owner_iota) & in_flight[k : k + 1, :]
        matches.append(hit)
        picked = picked + hit.astype(jnp.float32)
    row = lax.broadcasted_iota(jnp.int32, (tok_count, tok_count), 0)
    col = lax.broadcasted_iota(jnp.int32, (tok_count, tok_count), 1)
    later = (row < col).astype(jnp.bfloat16)
    before = jnp.dot(picked.astype(jnp.bfloat16), later, preferred_element_type=jnp.float32)
    targets = []
    for k in range(choices):
        rank = jnp.sum(jnp.where(matches[k], before, 0.0), axis=0, keepdims=True).astype(jnp.int32)
        keep = in_flight[k : k + 1, :] & (rank < CAP)
        target = jnp.where(keep, owner_of[k : k + 1, :] * CAP + rank, -1)
        targets.append(target)
    target_ref[...] = jnp.concatenate(targets, axis=0)
    owner_rank = jnp.where((picked > 0.0) & (before < CAP), before, -1.0)
    slot_iota = lax.broadcasted_iota(jnp.int32, (owners, CAP, tok_count), 1).astype(jnp.float32)
    chosen = (owner_rank[:, None, :] == slot_iota).astype(jnp.float32)
    chosen = chosen.reshape(slots, tok_count).astype(jnp.bfloat16)
    fetch.wait()
    width = tokens_vmem.shape[1]
    block = 1024
    for c in range(width // block):
        part = jnp.dot(
            chosen, tokens_vmem[:, c * block : (c + 1) * block], preferred_element_type=jnp.float32
        )
        out_ref[:, c * block : (c + 1) * block] = part.astype(out_ref.dtype)


def route_rows(ids_by_choice, tokens, owners):
    choices, tok_count = ids_by_choice.shape
    width = tokens.shape[1]
    slots = owners * CAP
    return pl.pallas_call(
        route_kernel,
        out_shape=(
            jax.ShapeDtypeStruct((slots, width), tokens.dtype),
            jax.ShapeDtypeStruct((choices, tok_count), jnp.int32),
        ),
        in_specs=[
            pl.BlockSpec(memory_space=pltpu.VMEM),
            pl.BlockSpec(memory_space=pl.ANY),
        ],
        out_specs=(
            pl.BlockSpec(memory_space=pltpu.VMEM),
            pl.BlockSpec(memory_space=pltpu.VMEM),
        ),
        scratch_shapes=[
            pltpu.VMEM((tok_count, width), tokens.dtype),
            pltpu.SemaphoreType.DMA((1,)),
        ],
        cost_estimate=pl.CostEstimate(
            flops=2 * slots * tok_count * width,
            transcendentals=0,
            bytes_accessed=2 * (slots * width + tok_count * width),
        ),
    )(ids_by_choice, tokens)


def per_device(tokens, expert_ids, route_weight, gate_weight, up_weight, down_weight):
    owners = lax.axis_size("expert")
    pair_count = lax.axis_size("pair")
    tok_count = tokens.shape[0]
    model_width = tokens.shape[1]
    per_owner = EXPERTS // owners
    outgoing, target_by_choice = route_rows(expert_ids.T, tokens, owners)
    target = target_by_choice.T
    outgoing = outgoing.reshape(owners, CAP, model_width)
    gate_matrix = gate_weight[0]
    upper_matrix = up_weight[0]
    down_matrix = down_weight[0]
    arrived = lax.all_to_all(outgoing, "expert", split_axis=0, concat_axis=0, tiled=True)
    item_count = arrived.shape[1]
    hidden, output = swiglu_rows(
        arrived.reshape(-1, model_width), gate_matrix, upper_matrix, down_matrix
    )
    results = output.reshape(owners, item_count, model_width)
    returned = lax.all_to_all(results, "expert", split_axis=0, concat_axis=0, tiled=True)
    returned_flat = returned.reshape(-1, model_width)
    slot_iota = lax.broadcasted_iota(jnp.int32, (1, 1, owners * CAP), 2)
    hits = target[:, :, None] == slot_iota
    combine_matrix = jnp.sum(jnp.where(hits, route_weight[:, :, None], 0.0), axis=1)
    weight_high, weight_low = split_bf16(combine_matrix)
    combined = combine_rows(weight_high, weight_low, returned_flat)
    hess_scale = 2.0 / (CAP * owners * pair_count)
    row_share = FF // pair_count
    pair_place = lax.axis_index("pair")
    hidden_wide = hidden.astype(jnp.float32)
    corner_part = lax.dot_general(
        hidden[:, :PANEL], hidden[:, :PANEL], (((0,), (0,)), ((), ())),
        preferred_element_type=jnp.float32,
    )
    square_part = jnp.broadcast_to(jnp.sum(hidden_wide * hidden_wide), (8, PANEL))
    pack = jnp.concatenate([corner_part, square_part], axis=0)
    pack_sum = pack
    for shift in range(1, pair_count):
        ring = [(i, (i + shift) % pair_count) for i in range(pair_count)]
        pack_sum = pack_sum + lax.ppermute(pack, "pair", ring)
    corner = pack_sum[:PANEL] * hess_scale
    damping = 0.01 * (pack_sum[PANEL, 0] * hess_scale) / FF
    lower_factor = jnp.linalg.cholesky(corner + damping * jnp.eye(PANEL, dtype=jnp.float32))
    gathered = [hidden]
    for shift in range(1, pair_count):
        ring = [(i, (i + shift) % pair_count) for i in range(pair_count)]
        gathered.append(lax.ppermute(hidden, "pair", ring))
    all_hidden = jnp.concatenate(gathered, axis=0)
    my_columns = lax.dynamic_slice_in_dim(all_hidden, pair_place * row_share, row_share, 1)
    my_rows = (
        lax.dot_general(
            my_columns, all_hidden, (((0,), (0,)), ((), ())), preferred_element_type=jnp.float32
        )
        * hess_scale
    )
    row_ids = pair_place * row_share + lax.broadcasted_iota(jnp.int32, (row_share, PANEL), 0)
    column_ids = lax.broadcasted_iota(jnp.int32, (row_share, PANEL), 1)
    leading = my_rows[:, :PANEL] + damping * (row_ids == column_ids).astype(jnp.float32)
    panel_rows = jax.scipy.linalg.solve_triangular(lower_factor, leading.T, lower=True).T
    return (combined, my_rows[None], panel_rows[None])


def solution(mesh):
    in_specs = (
        P(("expert", "pair"), None),
        P(("expert", "pair"), None),
        P(("expert", "pair"), None),
        P("expert", None, None),
        P("expert", None, None),
        P("expert", None, None),
    )
    out_specs = (P(("expert", "pair"), None), P("expert", "pair", None), P("expert", "pair", None))
    return jax.shard_map(
        per_device, mesh=mesh, in_specs=in_specs, out_specs=out_specs, check_vma=False
    )
```

```python
import jax
import jax.numpy as jnp
from jax import lax
from jax.sharding import PartitionSpec as P
from jax.experimental import pallas as pl
from jax.experimental.pallas import tpu as pltpu

EXPERTS = 128
FF = 768
PANEL = 128
CAP = 16


def swiglu_rows(flat_rows, gate_matrix, upper_matrix, down_matrix):
    gate_value = jnp.dot(flat_rows, gate_matrix, preferred_element_type=jnp.float32)
    upper_value = jnp.dot(flat_rows, upper_matrix, preferred_element_type=jnp.float32)
    hidden = (jax.nn.silu(gate_value) * upper_value).astype(jnp.bfloat16)
    output = jnp.dot(hidden, down_matrix, preferred_element_type=jnp.float32).astype(jnp.bfloat16)
    return (hidden, output)


def split_bf16(values):
    rounded = lax.reduce_precision(values, exponent_bits=8, mantissa_bits=7)
    return rounded.astype(jnp.bfloat16), (values - rounded).astype(jnp.bfloat16)


def combine_kernel(high_ref, low_ref, rows_ref, out_ref):
    rows = rows_ref[...]
    total = jnp.dot(high_ref[...], rows, preferred_element_type=jnp.float32)
    total = total + jnp.dot(low_ref[...], rows, preferred_element_type=jnp.float32)
    out_ref[...] = total.astype(out_ref.dtype)


def combine_rows(weight_high, weight_low, rows):
    tok_count, slot_count = weight_high.shape
    width = rows.shape[1]
    block = 2048
    return pl.pallas_call(
        combine_kernel,
        out_shape=jax.ShapeDtypeStruct((tok_count, width), jnp.bfloat16),
        grid=(width // block,),
        in_specs=[
            pl.BlockSpec((tok_count, slot_count), lambda j: (0, 0)),
            pl.BlockSpec((tok_count, slot_count), lambda j: (0, 0)),
            pl.BlockSpec((slot_count, block), lambda j: (0, j)),
        ],
        out_specs=pl.BlockSpec((tok_count, block), lambda j: (0, j)),
        cost_estimate=pl.CostEstimate(
            flops=4 * tok_count * slot_count * width,
            transcendentals=0,
            bytes_accessed=2 * (slot_count * width + tok_count * width + 2 * tok_count * slot_count),
        ),
    )(weight_high, weight_low, rows)


def route_kernel(ids_ref, tokens_hbm, out_ref, target_ref, tokens_vmem, copy_sem):
    fetch = pltpu.make_async_copy(tokens_hbm, tokens_vmem, copy_sem.at[0])
    fetch.start()
    choices, tok_count = ids_ref.shape
    slots = out_ref.shape[0]
    owners = slots // CAP
    per_owner = EXPERTS // owners
    ids = ids_ref[...]
    in_flight = (ids % per_owner) == 0
    owner_of = ids // per_owner
    owner_iota = lax.broadcasted_iota(jnp.int32, (owners, tok_count), 0)
    matches = []
    picked = jnp.zeros((owners, tok_count), jnp.float32)
    for k in range(choices):
        hit = (owner_of[k : k + 1, :] == owner_iota) & in_flight[k : k + 1, :]
        matches.append(hit)
        picked = picked + hit.astype(jnp.float32)
    row = lax.broadcasted_iota(jnp.int32, (tok_count, tok_count), 0)
    col = lax.broadcasted_iota(jnp.int32, (tok_count, tok_count), 1)
    later = (row < col).astype(jnp.bfloat16)
    before = jnp.dot(picked.astype(jnp.bfloat16), later, preferred_element_type=jnp.float32)
    targets = []
    for k in range(choices):
        rank = jnp.sum(jnp.where(matches[k], before, 0.0), axis=0, keepdims=True).astype(jnp.int32)
        keep = in_flight[k : k + 1, :] & (rank < CAP)
        target = jnp.where(keep, owner_of[k : k + 1, :] * CAP + rank, -1)
        targets.append(target)
    target_ref[...] = jnp.concatenate(targets, axis=0)
    owner_rank = jnp.where((picked > 0.0) & (before < CAP), before, -1.0)
    slot_iota = lax.broadcasted_iota(jnp.int32, (owners, CAP, tok_count), 1).astype(jnp.float32)
    chosen = (owner_rank[:, None, :] == slot_iota).astype(jnp.float32)
    chosen = chosen.reshape(slots, tok_count).astype(jnp.bfloat16)
    fetch.wait()
    width = tokens_vmem.shape[1]
    block = 1024
    for c in range(width // block):
        part = jnp.dot(
            chosen, tokens_vmem[:, c * block : (c + 1) * block], preferred_element_type=jnp.float32
        )
        out_ref[:, c * block : (c + 1) * block] = part.astype(out_ref.dtype)


def route_rows(ids_by_choice, tokens, owners):
    choices, tok_count = ids_by_choice.shape
    width = tokens.shape[1]
    slots = owners * CAP
    return pl.pallas_call(
        route_kernel,
        out_shape=(
            jax.ShapeDtypeStruct((slots, width), tokens.dtype),
            jax.ShapeDtypeStruct((choices, tok_count), jnp.int32),
        ),
        in_specs=[
            pl.BlockSpec(memory_space=pltpu.VMEM),
            pl.BlockSpec(memory_space=pl.ANY),
        ],
        out_specs=(
            pl.BlockSpec(memory_space=pltpu.VMEM),
            pl.BlockSpec(memory_space=pltpu.VMEM),
        ),
        scratch_shapes=[
            pltpu.VMEM((tok_count, width), tokens.dtype),
            pltpu.SemaphoreType.DMA((1,)),
        ],
        compiler_params=pltpu.CompilerParams(vmem_limit_bytes=48 * 1024 * 1024),
        cost_estimate=pl.CostEstimate(
            flops=2 * slots * tok_count * width,
            transcendentals=0,
            bytes_accessed=2 * (slots * width + tok_count * width),
        ),
    )(ids_by_choice, tokens)


def per_device(tokens, expert_ids, route_weight, gate_weight, up_weight, down_weight):
    owners = lax.axis_size("expert")
    pair_count = lax.axis_size("pair")
    tok_count = tokens.shape[0]
    model_width = tokens.shape[1]
    per_owner = EXPERTS // owners
    outgoing, target_by_choice = route_rows(expert_ids.T, tokens, owners)
    target = target_by_choice.T
    outgoing = outgoing.reshape(owners, CAP, model_width)
    gate_matrix = gate_weight[0]
    upper_matrix = up_weight[0]
    down_matrix = down_weight[0]
    arrived = lax.all_to_all(outgoing, "expert", split_axis=0, concat_axis=0, tiled=True)
    item_count = arrived.shape[1]
    hidden, output = swiglu_rows(
        arrived.reshape(-1, model_width), gate_matrix, upper_matrix, down_matrix
    )
    results = output.reshape(owners, item_count, model_width)
    returned = lax.all_to_all(results, "expert", split_axis=0, concat_axis=0, tiled=True)
    returned_flat = returned.reshape(-1, model_width)
    slot_iota = lax.broadcasted_iota(jnp.int32, (1, 1, owners * CAP), 2)
    hits = target[:, :, None] == slot_iota
    combine_matrix = jnp.sum(jnp.where(hits, route_weight[:, :, None], 0.0), axis=1)
    weight_high, weight_low = split_bf16(combine_matrix)
    combined = combine_rows(weight_high, weight_low, returned_flat)
    hess_scale = 2.0 / (CAP * owners * pair_count)
    row_share = FF // pair_count
    pair_place = lax.axis_index("pair")
    corner_part = lax.dot_general(
        hidden[:, :PANEL], hidden[:, :PANEL], (((0,), (0,)), ((), ())),
        preferred_element_type=jnp.float32,
    )
    held = lax.optimization_barrier(hidden).astype(jnp.float32)
    square_sum = jnp.sum(held * held)
    square_part = jnp.broadcast_to(square_sum, (8, PANEL))
    pack = jnp.concatenate([corner_part, square_part], axis=0)
    pack_sum = pack
    for shift in range(1, pair_count):
        ring = [(i, (i + shift) % pair_count) for i in range(pair_count)]
        pack_sum = pack_sum + lax.ppermute(pack, "pair", ring)
    corner = pack_sum[:PANEL] * hess_scale
    damping = 0.01 * (pack_sum[PANEL, 0] * hess_scale) / FF
    lower_factor = jnp.linalg.cholesky(corner + damping * jnp.eye(PANEL, dtype=jnp.float32))
    gathered = [hidden]
    for shift in range(1, pair_count):
        ring = [(i, (i + shift) % pair_count) for i in range(pair_count)]
        gathered.append(lax.ppermute(hidden, "pair", ring))
    all_hidden = jnp.concatenate(gathered, axis=0)
    my_columns = lax.dynamic_slice_in_dim(all_hidden, pair_place * row_share, row_share, 1)
    my_rows = (
        lax.dot_general(
            my_columns, all_hidden, (((0,), (0,)), ((), ())), preferred_element_type=jnp.float32
        )
        * hess_scale
    )
    row_ids = pair_place * row_share + lax.broadcasted_iota(jnp.int32, (row_share, PANEL), 0)
    column_ids = lax.broadcasted_iota(jnp.int32, (row_share, PANEL), 1)
    leading = my_rows[:, :PANEL] + damping * (row_ids == column_ids).astype(jnp.float32)
    panel_rows = jax.scipy.linalg.solve_triangular(lower_factor, leading.T, lower=True).T
    return (combined, my_rows[None], panel_rows[None])


def solution(mesh):
    in_specs = (
        P(("expert", "pair"), None),
        P(("expert", "pair"), None),
        P(("expert", "pair"), None),
        P("expert", None, None),
        P("expert", None, None),
        P("expert", None, None),
    )
    out_specs = (P(("expert", "pair"), None), P("expert", "pair", None), P("expert", "pair", None))
    return jax.shard_map(
        per_device, mesh=mesh, in_specs=in_specs, out_specs=out_specs, check_vma=False
    )
```

```python
import jax
import jax.numpy as jnp
from jax import lax
from jax.sharding import PartitionSpec as P
from jax.experimental import pallas as pl
from jax.experimental.pallas import tpu as pltpu

EXPERTS = 128
FF = 768
PANEL = 128
CAP = 16


def swiglu_rows(flat_rows, gate_matrix, upper_matrix, down_matrix):
    gate_value = jnp.dot(flat_rows, gate_matrix, preferred_element_type=jnp.float32)
    upper_value = jnp.dot(flat_rows, upper_matrix, preferred_element_type=jnp.float32)
    hidden = (jax.nn.silu(gate_value) * upper_value).astype(jnp.bfloat16)
    output = jnp.dot(hidden, down_matrix, preferred_element_type=jnp.float32).astype(jnp.bfloat16)
    return (hidden, output)


def split_bf16(values):
    rounded = lax.reduce_precision(values, exponent_bits=8, mantissa_bits=7)
    return rounded.astype(jnp.bfloat16), (values - rounded).astype(jnp.bfloat16)


def combine_kernel(high_ref, low_ref, rows_ref, out_ref):
    rows = rows_ref[...]
    total = jnp.dot(high_ref[...], rows, preferred_element_type=jnp.float32)
    total = total + jnp.dot(low_ref[...], rows, preferred_element_type=jnp.float32)
    out_ref[...] = total.astype(out_ref.dtype)


def combine_rows(weight_high, weight_low, rows):
    tok_count, slot_count = weight_high.shape
    width = rows.shape[1]
    block = 2048
    return pl.pallas_call(
        combine_kernel,
        out_shape=jax.ShapeDtypeStruct((tok_count, width), jnp.bfloat16),
        grid=(width // block,),
        in_specs=[
            pl.BlockSpec((tok_count, slot_count), lambda j: (0, 0)),
            pl.BlockSpec((tok_count, slot_count), lambda j: (0, 0)),
            pl.BlockSpec((slot_count, block), lambda j: (0, j)),
        ],
        out_specs=pl.BlockSpec((tok_count, block), lambda j: (0, j)),
        cost_estimate=pl.CostEstimate(
            flops=4 * tok_count * slot_count * width,
            transcendentals=0,
            bytes_accessed=2 * (slot_count * width + tok_count * width + 2 * tok_count * slot_count),
        ),
    )(weight_high, weight_low, rows)


def route_kernel(ids_ref, chosen_ref, target_ref):
    choices, tok_count = ids_ref.shape
    slots = chosen_ref.shape[1]
    owners = slots // CAP
    per_owner = EXPERTS // owners
    ids = ids_ref[...]
    in_flight = (ids % per_owner) == 0
    owner_of = ids // per_owner
    owner_iota = lax.broadcasted_iota(jnp.int32, (owners, tok_count), 0)
    matches = []
    picked = jnp.zeros((owners, tok_count), jnp.float32)
    for k in range(choices):
        hit = (owner_of[k : k + 1, :] == owner_iota) & in_flight[k : k + 1, :]
        matches.append(hit)
        picked = picked + hit.astype(jnp.float32)
    row = lax.broadcasted_iota(jnp.int32, (tok_count, tok_count), 0)
    col = lax.broadcasted_iota(jnp.int32, (tok_count, tok_count), 1)
    later = (row < col).astype(jnp.bfloat16)
    before = jnp.dot(picked.astype(jnp.bfloat16), later, preferred_element_type=jnp.float32)
    targets = []
    for k in range(choices):
        rank = jnp.sum(jnp.where(matches[k], before, 0.0), axis=0, keepdims=True).astype(jnp.int32)
        keep = in_flight[k : k + 1, :] & (rank < CAP)
        target = jnp.where(keep, owner_of[k : k + 1, :] * CAP + rank, -1)
        targets.append(target)
    target_ref[...] = jnp.concatenate(targets, axis=0)
    owner_rank = jnp.where((picked > 0.0) & (before < CAP), before, -1.0)
    slot_iota = lax.broadcasted_iota(jnp.int32, (owners, CAP, tok_count), 1).astype(jnp.float32)
    chosen = (owner_rank[:, None, :] == slot_iota).astype(jnp.float32)
    chosen_ref[...] = chosen.reshape(slots, tok_count).T.astype(chosen_ref.dtype)


def route_rows(ids_by_choice, tokens, owners):
    choices, tok_count = ids_by_choice.shape
    slots = owners * CAP
    chosen, target = pl.pallas_call(
        route_kernel,
        out_shape=(
            jax.ShapeDtypeStruct((tok_count, slots), jnp.bfloat16),
            jax.ShapeDtypeStruct((choices, tok_count), jnp.int32),
        ),
        in_specs=[pl.BlockSpec(memory_space=pltpu.VMEM)],
        out_specs=(
            pl.BlockSpec(memory_space=pltpu.VMEM),
            pl.BlockSpec(memory_space=pltpu.VMEM),
        ),
        cost_estimate=pl.CostEstimate(
            flops=2 * owners * tok_count * tok_count, transcendentals=0, bytes_accessed=4 * slots * tok_count
        ),
    )(ids_by_choice)
    outgoing = lax.dot_general(
        chosen, tokens, (((0,), (0,)), ((), ())), preferred_element_type=jnp.float32
    ).astype(tokens.dtype)
    return outgoing, target


def per_device(tokens, expert_ids, route_weight, gate_weight, up_weight, down_weight):
    owners = lax.axis_size("expert")
    pair_count = lax.axis_size("pair")
    tok_count = tokens.shape[0]
    model_width = tokens.shape[1]
    per_owner = EXPERTS // owners
    outgoing, target_by_choice = route_rows(expert_ids.T, tokens, owners)
    target = target_by_choice.T
    outgoing = outgoing.reshape(owners, CAP, model_width)
    gate_matrix = gate_weight[0]
    upper_matrix = up_weight[0]
    down_matrix = down_weight[0]
    arrived = lax.all_to_all(outgoing, "expert", split_axis=0, concat_axis=0, tiled=True)
    item_count = arrived.shape[1]
    hidden, output = swiglu_rows(
        arrived.reshape(-1, model_width), gate_matrix, upper_matrix, down_matrix
    )
    results = output.reshape(owners, item_count, model_width)
    returned = lax.all_to_all(results, "expert", split_axis=0, concat_axis=0, tiled=True)
    returned_flat = returned.reshape(-1, model_width)
    slot_iota = lax.broadcasted_iota(jnp.int32, (1, 1, owners * CAP), 2)
    hits = target[:, :, None] == slot_iota
    combine_matrix = jnp.sum(jnp.where(hits, route_weight[:, :, None], 0.0), axis=1)
    weight_high, weight_low = split_bf16(combine_matrix)
    combined = combine_rows(weight_high, weight_low, returned_flat)
    hess_scale = 2.0 / (CAP * owners * pair_count)
    row_share = FF // pair_count
    pair_place = lax.axis_index("pair")
    corner_part = lax.dot_general(
        hidden[:, :PANEL], hidden[:, :PANEL], (((0,), (0,)), ((), ())),
        preferred_element_type=jnp.float32,
    )
    held = lax.optimization_barrier(hidden).astype(jnp.float32)
    square_sum = jnp.sum(held * held)
    square_part = jnp.broadcast_to(square_sum, (8, PANEL))
    pack = jnp.concatenate([corner_part, square_part], axis=0)
    pack_sum = pack
    for shift in range(1, pair_count):
        ring = [(i, (i + shift) % pair_count) for i in range(pair_count)]
        pack_sum = pack_sum + lax.ppermute(pack, "pair", ring)
    corner = pack_sum[:PANEL] * hess_scale
    damping = 0.01 * (pack_sum[PANEL, 0] * hess_scale) / FF
    lower_factor = jnp.linalg.cholesky(corner + damping * jnp.eye(PANEL, dtype=jnp.float32))
    gathered = [hidden]
    for shift in range(1, pair_count):
        ring = [(i, (i + shift) % pair_count) for i in range(pair_count)]
        gathered.append(lax.ppermute(hidden, "pair", ring))
    all_hidden = jnp.concatenate(gathered, axis=0)
    my_columns = lax.dynamic_slice_in_dim(all_hidden, pair_place * row_share, row_share, 1)
    my_rows = (
        lax.dot_general(
            my_columns, all_hidden, (((0,), (0,)), ((), ())), preferred_element_type=jnp.float32
        )
        * hess_scale
    )
    row_ids = pair_place * row_share + lax.broadcasted_iota(jnp.int32, (row_share, PANEL), 0)
    column_ids = lax.broadcasted_iota(jnp.int32, (row_share, PANEL), 1)
    leading = my_rows[:, :PANEL] + damping * (row_ids == column_ids).astype(jnp.float32)
    panel_rows = jax.scipy.linalg.solve_triangular(lower_factor, leading.T, lower=True).T
    return (combined, my_rows[None], panel_rows[None])


def solution(mesh):
    in_specs = (
        P(("expert", "pair"), None),
        P(("expert", "pair"), None),
        P(("expert", "pair"), None),
        P("expert", None, None),
        P("expert", None, None),
        P("expert", None, None),
    )
    out_specs = (P(("expert", "pair"), None), P("expert", "pair", None), P("expert", "pair", None))
    return jax.shard_map(
        per_device, mesh=mesh, in_specs=in_specs, out_specs=out_specs, check_vma=False
    )
```

```python
import jax
import jax.numpy as jnp
from jax import lax
from jax.sharding import PartitionSpec as P
from jax.experimental import pallas as pl
from jax.experimental.pallas import tpu as pltpu

EXPERTS = 128
FF = 768
PANEL = 128
CAP = 16


def swiglu_rows(flat_rows, gate_matrix, upper_matrix, down_matrix):
    gate_value = jnp.dot(flat_rows, gate_matrix, preferred_element_type=jnp.float32)
    upper_value = jnp.dot(flat_rows, upper_matrix, preferred_element_type=jnp.float32)
    hidden = (jax.nn.silu(gate_value) * upper_value).astype(jnp.bfloat16)
    output = jnp.dot(hidden, down_matrix, preferred_element_type=jnp.float32).astype(jnp.bfloat16)
    return (hidden, output)


def split_bf16(values):
    rounded = lax.reduce_precision(values, exponent_bits=8, mantissa_bits=7)
    return rounded.astype(jnp.bfloat16), (values - rounded).astype(jnp.bfloat16)


def combine_kernel(high_ref, low_ref, rows_ref, out_ref):
    rows = rows_ref[...]
    total = jnp.dot(high_ref[...], rows, preferred_element_type=jnp.float32)
    total = total + jnp.dot(low_ref[...], rows, preferred_element_type=jnp.float32)
    out_ref[...] = total.astype(out_ref.dtype)


def combine_rows(weight_high, weight_low, rows):
    tok_count, slot_count = weight_high.shape
    width = rows.shape[1]
    block = 2048
    return pl.pallas_call(
        combine_kernel,
        out_shape=jax.ShapeDtypeStruct((tok_count, width), jnp.bfloat16),
        grid=(width // block,),
        in_specs=[
            pl.BlockSpec((tok_count, slot_count), lambda j: (0, 0)),
            pl.BlockSpec((tok_count, slot_count), lambda j: (0, 0)),
            pl.BlockSpec((slot_count, block), lambda j: (0, j)),
        ],
        out_specs=pl.BlockSpec((tok_count, block), lambda j: (0, j)),
        cost_estimate=pl.CostEstimate(
            flops=4 * tok_count * slot_count * width,
            transcendentals=0,
            bytes_accessed=2 * (slot_count * width + tok_count * width + 2 * tok_count * slot_count),
        ),
    )(weight_high, weight_low, rows)


def route_kernel(ids_ref, tokens_ref, out_ref, target_ref, chosen_ref):
    @pl.when(pl.program_id(0) == 0)
    def _():
        choices, tok_count = ids_ref.shape
        slots = out_ref.shape[0]
        owners = slots // CAP
        per_owner = EXPERTS // owners
        ids = ids_ref[...]
        in_flight = (ids % per_owner) == 0
        owner_of = ids // per_owner
        owner_iota = lax.broadcasted_iota(jnp.int32, (owners, tok_count), 0)
        matches = []
        picked = jnp.zeros((owners, tok_count), jnp.float32)
        for k in range(choices):
            hit = (owner_of[k : k + 1, :] == owner_iota) & in_flight[k : k + 1, :]
            matches.append(hit)
            picked = picked + hit.astype(jnp.float32)
        row = lax.broadcasted_iota(jnp.int32, (tok_count, tok_count), 0)
        col = lax.broadcasted_iota(jnp.int32, (tok_count, tok_count), 1)
        later = (row < col).astype(jnp.bfloat16)
        before = jnp.dot(picked.astype(jnp.bfloat16), later, preferred_element_type=jnp.float32)
        targets = []
        for k in range(choices):
            rank = jnp.sum(jnp.where(matches[k], before, 0.0), axis=0, keepdims=True)
            rank = rank.astype(jnp.int32)
            keep = in_flight[k : k + 1, :] & (rank < CAP)
            target = jnp.where(keep, owner_of[k : k + 1, :] * CAP + rank, -1)
            targets.append(target)
        target_ref[...] = jnp.concatenate(targets, axis=0)
        owner_rank = jnp.where((picked > 0.0) & (before < CAP), before, -1.0)
        slot_iota = lax.broadcasted_iota(jnp.int32, (owners, CAP, tok_count), 1).astype(jnp.float32)
        chosen = (owner_rank[:, None, :] == slot_iota).astype(jnp.float32)
        chosen_ref[...] = chosen.reshape(slots, tok_count).astype(chosen_ref.dtype)

    part = jnp.dot(chosen_ref[...], tokens_ref[...], preferred_element_type=jnp.float32)
    out_ref[...] = part.astype(out_ref.dtype)


def route_rows(ids_by_choice, tokens, owners):
    choices, tok_count = ids_by_choice.shape
    width = tokens.shape[1]
    slots = owners * CAP
    block = width // 2
    return pl.pallas_call(
        route_kernel,
        out_shape=(
            jax.ShapeDtypeStruct((slots, width), tokens.dtype),
            jax.ShapeDtypeStruct((choices, tok_count), jnp.int32),
        ),
        grid=(width // block,),
        in_specs=[
            pl.BlockSpec((choices, tok_count), lambda j: (0, 0)),
            pl.BlockSpec((tok_count, block), lambda j: (0, j)),
        ],
        out_specs=(
            pl.BlockSpec((slots, block), lambda j: (0, j)),
            pl.BlockSpec((choices, tok_count), lambda j: (0, 0)),
        ),
        scratch_shapes=[pltpu.VMEM((slots, tok_count), jnp.bfloat16)],
        cost_estimate=pl.CostEstimate(
            flops=2 * slots * tok_count * width,
            transcendentals=0,
            bytes_accessed=2 * (slots * width + tok_count * width),
        ),
    )(ids_by_choice, tokens)


def per_device(tokens, expert_ids, route_weight, gate_weight, up_weight, down_weight):
    owners = lax.axis_size("expert")
    pair_count = lax.axis_size("pair")
    tok_count = tokens.shape[0]
    model_width = tokens.shape[1]
    per_owner = EXPERTS // owners
    outgoing, target_by_choice = route_rows(expert_ids.T, tokens, owners)
    target = target_by_choice.T
    outgoing = outgoing.reshape(owners, CAP, model_width)
    gate_matrix = gate_weight[0]
    upper_matrix = up_weight[0]
    down_matrix = down_weight[0]
    arrived = lax.all_to_all(outgoing, "expert", split_axis=0, concat_axis=0, tiled=True)
    item_count = arrived.shape[1]
    hidden, output = swiglu_rows(
        arrived.reshape(-1, model_width), gate_matrix, upper_matrix, down_matrix
    )
    results = output.reshape(owners, item_count, model_width)
    returned = lax.all_to_all(results, "expert", split_axis=0, concat_axis=0, tiled=True)
    returned_flat = returned.reshape(-1, model_width)
    slot_iota = lax.broadcasted_iota(jnp.int32, (1, 1, owners * CAP), 2)
    hits = target[:, :, None] == slot_iota
    combine_matrix = jnp.sum(jnp.where(hits, route_weight[:, :, None], 0.0), axis=1)
    weight_high, weight_low = split_bf16(combine_matrix)
    combined = combine_rows(weight_high, weight_low, returned_flat)
    hess_scale = 2.0 / (CAP * owners * pair_count)
    row_share = FF // pair_count
    pair_place = lax.axis_index("pair")
    corner_part = lax.dot_general(
        hidden[:, :PANEL], hidden[:, :PANEL], (((0,), (0,)), ((), ())),
        preferred_element_type=jnp.float32,
    )
    held = lax.optimization_barrier(hidden).astype(jnp.float32)
    square_sum = jnp.sum(held * held)
    square_part = jnp.broadcast_to(square_sum, (8, PANEL))
    pack = jnp.concatenate([corner_part, square_part], axis=0)
    pack_sum = pack
    for shift in range(1, pair_count):
        ring = [(i, (i + shift) % pair_count) for i in range(pair_count)]
        pack_sum = pack_sum + lax.ppermute(pack, "pair", ring)
    corner = pack_sum[:PANEL] * hess_scale
    damping = 0.01 * (pack_sum[PANEL, 0] * hess_scale) / FF
    lower_factor = jnp.linalg.cholesky(corner + damping * jnp.eye(PANEL, dtype=jnp.float32))
    gathered = [hidden]
    for shift in range(1, pair_count):
        ring = [(i, (i + shift) % pair_count) for i in range(pair_count)]
        gathered.append(lax.ppermute(hidden, "pair", ring))
    all_hidden = jnp.concatenate(gathered, axis=0)
    my_columns = lax.dynamic_slice_in_dim(all_hidden, pair_place * row_share, row_share, 1)
    my_rows = (
        lax.dot_general(
            my_columns, all_hidden, (((0,), (0,)), ((), ())), preferred_element_type=jnp.float32
        )
        * hess_scale
    )
    row_ids = pair_place * row_share + lax.broadcasted_iota(jnp.int32, (row_share, PANEL), 0)
    column_ids = lax.broadcasted_iota(jnp.int32, (row_share, PANEL), 1)
    leading = my_rows[:, :PANEL] + damping * (row_ids == column_ids).astype(jnp.float32)
    panel_rows = jax.scipy.linalg.solve_triangular(lower_factor, leading.T, lower=True).T
    return (combined, my_rows[None], panel_rows[None])


def solution(mesh):
    in_specs = (
        P(("expert", "pair"), None),
        P(("expert", "pair"), None),
        P(("expert", "pair"), None),
        P("expert", None, None),
        P("expert", None, None),
        P("expert", None, None),
    )
    out_specs = (P(("expert", "pair"), None), P("expert", "pair", None), P("expert", "pair", None))
    return jax.shard_map(
        per_device, mesh=mesh, in_specs=in_specs, out_specs=out_specs, check_vma=False
    )
```

```python
import jax
import jax.numpy as jnp
from jax import lax
from jax.sharding import PartitionSpec as P
from jax.experimental import pallas as pl
from jax.experimental.pallas import tpu as pltpu

EXPERTS = 128
FF = 768
PANEL = 128
CAP = 16


def swiglu_rows(flat_rows, gate_matrix, upper_matrix, down_matrix):
    gate_value = jnp.dot(flat_rows, gate_matrix, preferred_element_type=jnp.float32)
    upper_value = jnp.dot(flat_rows, upper_matrix, preferred_element_type=jnp.float32)
    hidden = (jax.nn.silu(gate_value) * upper_value).astype(jnp.bfloat16)
    output = down_rows(hidden, down_matrix)
    return (hidden, output)


def down_kernel(hidden_ref, down_hbm, out_hbm, weights, staging, load_sem, store_sem):
    width = down_hbm.shape[1]
    block = 1024
    steps = width // block
    loads = [
        pltpu.make_async_copy(
            down_hbm.at[:, pl.ds(c * block, block)], weights.at[c % 2], load_sem.at[c % 2]
        )
        for c in range(steps)
    ]
    loads[0].start()
    hidden = hidden_ref[...]
    stores = []
    for c in range(steps):
        slot = c % 2
        loads[c].wait()
        if c + 1 < steps:
            loads[c + 1].start()
        if c >= 2:
            stores[c - 2].wait()
        part = jnp.dot(hidden, weights[slot], preferred_element_type=jnp.float32)
        staging[slot] = part.astype(staging.dtype)
        store = pltpu.make_async_copy(
            staging.at[slot], out_hbm.at[:, pl.ds(c * block, block)], store_sem.at[slot]
        )
        store.start()
        stores.append(store)
    for store in stores[-2:]:
        store.wait()


def down_rows(hidden, down_matrix):
    rows, inner = hidden.shape
    width = down_matrix.shape[1]
    return pl.pallas_call(
        down_kernel,
        out_shape=jax.ShapeDtypeStruct((rows, width), jnp.bfloat16),
        in_specs=[pl.BlockSpec(memory_space=pltpu.VMEM), pl.BlockSpec(memory_space=pl.ANY)],
        out_specs=pl.BlockSpec(memory_space=pl.ANY),
        scratch_shapes=[
            pltpu.VMEM((2, inner, 1024), jnp.bfloat16),
            pltpu.VMEM((2, rows, 1024), jnp.bfloat16),
            pltpu.SemaphoreType.DMA((2,)),
            pltpu.SemaphoreType.DMA((2,)),
        ],
        cost_estimate=pl.CostEstimate(
            flops=2 * rows * inner * width,
            transcendentals=0,
            bytes_accessed=2 * (rows * inner + inner * width + rows * width),
        ),
    )(hidden, down_matrix)


def split_bf16(values):
    rounded = lax.reduce_precision(values, exponent_bits=8, mantissa_bits=7)
    return rounded.astype(jnp.bfloat16), (values - rounded).astype(jnp.bfloat16)


def combine_kernel(high_ref, low_ref, rows_ref, out_ref):
    rows = rows_ref[...]
    total = jnp.dot(high_ref[...], rows, preferred_element_type=jnp.float32)
    total = total + jnp.dot(low_ref[...], rows, preferred_element_type=jnp.float32)
    out_ref[...] = total.astype(out_ref.dtype)


def combine_rows(weight_high, weight_low, rows):
    tok_count, slot_count = weight_high.shape
    width = rows.shape[1]
    block = 2048
    return pl.pallas_call(
        combine_kernel,
        out_shape=jax.ShapeDtypeStruct((tok_count, width), jnp.bfloat16),
        grid=(width // block,),
        in_specs=[
            pl.BlockSpec((tok_count, slot_count), lambda j: (0, 0)),
            pl.BlockSpec((tok_count, slot_count), lambda j: (0, 0)),
            pl.BlockSpec((slot_count, block), lambda j: (0, j)),
        ],
        out_specs=pl.BlockSpec((tok_count, block), lambda j: (0, j)),
        compiler_params=pltpu.CompilerParams(),
        cost_estimate=pl.CostEstimate(
            flops=4 * tok_count * slot_count * width,
            transcendentals=0,
            bytes_accessed=2 * (slot_count * width + tok_count * width + 2 * tok_count * slot_count),
        ),
    )(weight_high, weight_low, rows)


def route_kernel(ids_ref, tokens_hbm, out_ref, target_ref, tokens_vmem, copy_sem):
    fetch = pltpu.make_async_copy(tokens_hbm, tokens_vmem, copy_sem.at[0])
    fetch.start()
    choices, tok_count = ids_ref.shape
    slots = out_ref.shape[0]
    owners = slots // CAP
    per_owner = EXPERTS // owners
    ids = ids_ref[...]
    in_flight = (ids % per_owner) == 0
    owner_of = ids // per_owner
    owner_iota = lax.broadcasted_iota(jnp.int32, (owners, tok_count), 0)
    matches = []
    picked = jnp.zeros((owners, tok_count), jnp.float32)
    for k in range(choices):
        hit = (owner_of[k : k + 1, :] == owner_iota) & in_flight[k : k + 1, :]
        matches.append(hit)
        picked = picked + hit.astype(jnp.float32)
    row = lax.broadcasted_iota(jnp.int32, (tok_count, tok_count), 0)
    col = lax.broadcasted_iota(jnp.int32, (tok_count, tok_count), 1)
    later = (row < col).astype(jnp.bfloat16)
    before = jnp.dot(picked.astype(jnp.bfloat16), later, preferred_element_type=jnp.float32)
    targets = []
    for k in range(choices):
        rank = jnp.sum(jnp.where(matches[k], before, 0.0), axis=0, keepdims=True).astype(jnp.int32)
        keep = in_flight[k : k + 1, :] & (rank < CAP)
        target = jnp.where(keep, owner_of[k : k + 1, :] * CAP + rank, -1)
        targets.append(target)
    target_ref[...] = jnp.concatenate(targets, axis=0)
    owner_rank = jnp.where((picked > 0.0) & (before < CAP), before, -1.0)
    slot_iota = lax.broadcasted_iota(jnp.int32, (owners, CAP, tok_count), 1).astype(jnp.float32)
    chosen = (owner_rank[:, None, :] == slot_iota).astype(jnp.float32)
    chosen = chosen.reshape(slots, tok_count).astype(jnp.bfloat16)
    fetch.wait()
    width = tokens_vmem.shape[1]
    block = 1024
    for c in range(width // block):
        part = jnp.dot(
            chosen, tokens_vmem[:, c * block : (c + 1) * block], preferred_element_type=jnp.float32
        )
        out_ref[:, c * block : (c + 1) * block] = part.astype(out_ref.dtype)


def route_rows(ids_by_choice, tokens, owners):
    choices, tok_count = ids_by_choice.shape
    width = tokens.shape[1]
    slots = owners * CAP
    return pl.pallas_call(
        route_kernel,
        out_shape=(
            jax.ShapeDtypeStruct((slots, width), tokens.dtype),
            jax.ShapeDtypeStruct((choices, tok_count), jnp.int32),
        ),
        in_specs=[
            pl.BlockSpec(memory_space=pltpu.VMEM),
            pl.BlockSpec(memory_space=pl.ANY),
        ],
        out_specs=(
            pl.BlockSpec(memory_space=pltpu.VMEM),
            pl.BlockSpec(memory_space=pltpu.VMEM),
        ),
        scratch_shapes=[
            pltpu.VMEM((tok_count, width), tokens.dtype),
            pltpu.SemaphoreType.DMA((1,)),
        ],
        compiler_params=pltpu.CompilerParams(
            vmem_limit_bytes=48 * 1024 * 1024
        ),
        cost_estimate=pl.CostEstimate(
            flops=2 * slots * tok_count * width,
            transcendentals=0,
            bytes_accessed=2 * (slots * width + tok_count * width),
        ),
    )(ids_by_choice, tokens)


def per_device(tokens, expert_ids, route_weight, gate_weight, up_weight, down_weight):
    owners = lax.axis_size("expert")
    pair_count = lax.axis_size("pair")
    tok_count = tokens.shape[0]
    model_width = tokens.shape[1]
    per_owner = EXPERTS // owners
    outgoing, target_by_choice = route_rows(expert_ids.T, tokens, owners)
    target = target_by_choice.T
    outgoing = outgoing.reshape(owners, CAP, model_width)
    gate_matrix = gate_weight[0]
    upper_matrix = up_weight[0]
    down_matrix = down_weight[0]
    arrived = lax.all_to_all(outgoing, "expert", split_axis=0, concat_axis=0, tiled=True)
    item_count = arrived.shape[1]
    hidden, output = swiglu_rows(
        arrived.reshape(-1, model_width), gate_matrix, upper_matrix, down_matrix
    )
    results = output.reshape(owners, item_count, model_width)
    returned = lax.all_to_all(results, "expert", split_axis=0, concat_axis=0, tiled=True)
    returned_flat = returned.reshape(-1, model_width)
    slot_iota = lax.broadcasted_iota(jnp.int32, (1, 1, owners * CAP), 2)
    hits = target[:, :, None] == slot_iota
    combine_matrix = jnp.sum(jnp.where(hits, route_weight[:, :, None], 0.0), axis=1)
    weight_high, weight_low = split_bf16(combine_matrix)
    combined = combine_rows(weight_high, weight_low, returned_flat)
    hess_scale = 2.0 / (CAP * owners * pair_count)
    row_share = FF // pair_count
    pair_place = lax.axis_index("pair")
    corner_part = lax.dot_general(
        hidden[:, :PANEL], hidden[:, :PANEL], (((0,), (0,)), ((), ())),
        preferred_element_type=jnp.float32,
    )
    held = lax.optimization_barrier(hidden).astype(jnp.float32)
    square_sum = jnp.sum(held * held)
    square_part = jnp.broadcast_to(square_sum, (8, PANEL))
    pack = jnp.concatenate([corner_part, square_part], axis=0)
    pack_sum = pack
    for shift in range(1, pair_count):
        ring = [(i, (i + shift) % pair_count) for i in range(pair_count)]
        pack_sum = pack_sum + lax.ppermute(pack, "pair", ring)
    corner = pack_sum[:PANEL] * hess_scale
    damping = 0.01 * (pack_sum[PANEL, 0] * hess_scale) / FF
    lower_factor = jnp.linalg.cholesky(corner + damping * jnp.eye(PANEL, dtype=jnp.float32))
    gathered = [hidden]
    for shift in range(1, pair_count):
        ring = [(i, (i + shift) % pair_count) for i in range(pair_count)]
        gathered.append(lax.ppermute(hidden, "pair", ring))
    all_hidden = jnp.concatenate(gathered, axis=0)
    my_columns = lax.dynamic_slice_in_dim(all_hidden, pair_place * row_share, row_share, 1)
    my_rows = (
        lax.dot_general(
            my_columns, all_hidden, (((0,), (0,)), ((), ())), preferred_element_type=jnp.float32
        )
        * hess_scale
    )
    row_ids = pair_place * row_share + lax.broadcasted_iota(jnp.int32, (row_share, PANEL), 0)
    column_ids = lax.broadcasted_iota(jnp.int32, (row_share, PANEL), 1)
    leading = my_rows[:, :PANEL] + damping * (row_ids == column_ids).astype(jnp.float32)
    panel_rows = jax.scipy.linalg.solve_triangular(lower_factor, leading.T, lower=True).T
    return (combined, my_rows[None], panel_rows[None])


def solution(mesh):
    in_specs = (
        P(("expert", "pair"), None),
        P(("expert", "pair"), None),
        P(("expert", "pair"), None),
        P("expert", None, None),
        P("expert", None, None),
        P("expert", None, None),
    )
    out_specs = (P(("expert", "pair"), None), P("expert", "pair", None), P("expert", "pair", None))
    return jax.shard_map(
        per_device, mesh=mesh, in_specs=in_specs, out_specs=out_specs, check_vma=False
    )
```
